128 devices in a mesh: gx: 16 (over x_hi, y, core), gy: 8 (over z, x_lo).
Axes of the slice: x: 4 (x_hi: 2, x_lo: 2; x = x_hi * 2 + x_lo), y: 4, z: 4, core: 2. Of those that a mesh axis runs over, the one named last changes fastest.
Arguments:
- element_blocks: bfloat16 [96, 64, 480, 480], P('gx', 'gy')
- mortar_projection: float32 [4, 80, 80], replicated
- face_sources: float32 [96, 64, 3, 1280], P('gx', 'gy'), may hold values from -6 to 6
- coarse_sources: float32 [512, 8, 1280], P('gx', 'gy'), may hold values from -6 to 6
- parent_slot: int32 [96, 64], P('gx', 'gy'), may hold values from 0 to 511, as said below
- child_position: int32 [96, 64], P('gx', 'gy'), may hold values from 0 to 3, as said below
- live_count: int32 [16, 8], P('gx', 'gy'), may hold values from 24 to 48, as said below
Outputs:
- face_traces: float32 [96, 64, 3, 1280], P('gx', 'gy')
- coarse_traces: float32 [512, 8, 1280], P('gx', 'gy')
The draws below stay inside these ranges and needn't reach their ends.
Inputs may be any that keep to these rules, and one draw needn't show every extreme that they name: `parent_slot`: the four elements of each aligned 2 x 2 block of one device's tile share one value s; blocks in one column of devices along gy have distinct values. s // 32 is the owner's index along gx, and s mod 32 lies in [a * 2, (a + 1) * 2) where a is the gx index of the block's device. One device's blocks have at most 2 with one owner, and exactly 2 with some owner; in every column one owner holds 2 blocks of each device of the column. `child_position`: the four elements of each aligned 2 x 2 block of one device's tile hold 0, 1, 2 and 3 in some order. `live_count`: some device has all of its elements live.
All inputs are finite; a program needn't handle non-finite values.
Results may differ from the reference program's by a relative error of at most 0.0012.
Values sent between devices are 32-bit elements; how exact they have to be, the bound alone decides.
No kernel may reach another device: no remote copies, remote signals or barrier semaphores. Data moves between devices by JAX's collectives and lax.ppermute only.
A program may use at most 192 MiB of HBM per device.

```python
import math
import jax
import jax.numpy as jnp
from jax import lax

FD = 80
FUNC = 16
BLOCK = 480
ELX = 6
ELY = 8
ITERS = 4
CAP = 2
OWN = 32
NXE = 96
NYE = 64
COARSE = 512
N_GX = 16
N_GY = 8


def draw_element_blocks(key, part):
    key_noise, key_diag = jax.random.split(jax.random.fold_in(key, 5))
    shape = (NXE, NYE, BLOCK, BLOCK)
    identity = (lax.broadcasted_iota(jnp.int32, (BLOCK, BLOCK), 0) == lax.broadcasted_iota(jnp.int32, (BLOCK, BLOCK), 1)).astype(jnp.float32)
    noise = jax.random.normal(key_noise, shape, jnp.float32) * (0.14 / math.sqrt(BLOCK))
    diagonal = jax.random.uniform(key_diag, (NXE, NYE, BLOCK), jnp.float32, 0.4, 0.8)
    return (noise + diagonal[..., None] * identity).astype(jnp.bfloat16)


def draw_mortar_projection(key, part):
    key_noise, key_diag = jax.random.split(jax.random.fold_in(key, 7))
    identity = (lax.broadcasted_iota(jnp.int32, (FD, FD), 0) == lax.broadcasted_iota(jnp.int32, (FD, FD), 1)).astype(jnp.float32)
    noise = jax.random.normal(key_noise, (4, FD, FD), jnp.float32) * (0.12 / math.sqrt(FD))
    diagonal = jax.random.uniform(key_diag, (4, FD), jnp.float32, 0.45, 0.65)
    return noise + diagonal[..., None] * identity


def expand_blocks(grid):
    moved = jnp.transpose(grid, (0, 2, 1, 3))[:, :, None, :, :, None]
    full = jnp.broadcast_to(moved, (N_GX, ELX // 2, 2, N_GY, ELY // 2, 2))
    return full.reshape(NXE, NYE)


def draw_parent_slot(key, part):
    groups = ELX * ELY // 4
    key_hot, key_rest = jax.random.split(jax.random.fold_in(key, 11))
    key_hot, key_column = jax.random.split(key_hot)
    hottest = jax.random.randint(key_hot, (N_GY,), 0, N_GX)
    last_column = jax.random.randint(key_column, (), 0, N_GY)
    hottest = jnp.where(jnp.arange(N_GY, dtype=jnp.int32) == last_column, N_GX - 1, hottest).astype(jnp.int32)
    device_keys = jax.random.split(key_rest, N_GX * N_GY)
    flat_ids = jnp.arange(N_GX * N_GY, dtype=jnp.int32)
    source_ids = flat_ids // N_GY
    hot_ids = hottest[flat_ids % N_GY]

    def one_device(device_key, source, hot_owner):
        key_order, key_pairs, key_shuffle = jax.random.split(device_key, 3)
        scores = jax.random.permutation(key_order, N_GX).astype(jnp.int32)
        scores = jnp.where(jnp.arange(N_GX, dtype=jnp.int32) == hot_owner, -1, scores)
        order = jnp.argsort(scores, stable=True).astype(jnp.int32)
        doubled = jax.random.randint(key_pairs, (), max(1, groups - N_GX), groups // 2 + 1)
        entry = jnp.arange(groups, dtype=jnp.int32)
        first_part = entry < 2 * doubled
        ranked = jnp.where(first_part, entry // 2, entry - doubled)
        copy_index = jnp.where(first_part, entry % 2, 0)
        slot_values = (order[ranked] * OWN + source * CAP + copy_index).astype(jnp.int32)
        shuffle = jax.random.permutation(key_shuffle, groups)
        return jnp.zeros((groups,), jnp.int32).at[shuffle].set(slot_values)
    flat = jax.vmap(one_device)(device_keys, source_ids, hot_ids)
    return expand_blocks(flat.reshape(N_GX, N_GY, ELX // 2, ELY // 2)).astype(jnp.int32)


def draw_child_position(key, part):
    total = N_GX * N_GY * (ELX // 2) * (ELY // 2)
    block_keys = jax.random.split(jax.random.fold_in(key, 23), total)
    orders = jax.vmap(lambda block_key: jax.random.permutation(block_key, 4))(block_keys)
    grid = orders.reshape(N_GX, N_GY, ELX // 2, ELY // 2, 2, 2)
    moved = jnp.transpose(grid, (0, 2, 4, 1, 3, 5))
    return moved.reshape(NXE, NYE).astype(jnp.int32)


def draw_live_count(key, part):
    most = ELX * ELY
    key_counts, key_full = jax.random.split(jax.random.fold_in(key, 37))
    counts = jax.random.randint(key_counts, (N_GX * N_GY,), most // 2, most + 1)
    fullest = jax.random.randint(key_full, (), 0, N_GX * N_GY)
    counts = jnp.where(jnp.arange(N_GX * N_GY) == fullest, most, counts)
    return counts.reshape(N_GX, N_GY).astype(jnp.int32)


def levels(own_key, shape, shards, least, high):
    level, own = 1.0, jax.random.fold_in(own_key, 6)
    for position, shards_of in shards:
        heights = jnp.exp(jax.random.uniform(jax.random.fold_in(own, position), (shards_of,), jnp.float32, least / len(shards), high / len(shards)))
        level = level * jnp.repeat(heights, shape[position] // shards_of).reshape([-1 if axis == position else 1 for axis in range(len(shape))])
    return level


def centred(own_key, extent, deviation, bound, pieces=(), kind=jnp.bfloat16):
    entries = jax.random.normal(own_key, extent, jnp.float32) * deviation
    if len(pieces) > 0:
        entries = levels(own_key, extent, pieces, -0.22, 0.18) * entries
    return jnp.clip(entries, min=-bound, max=bound).astype(kind)


def setup_inputs(seed: int = 0) -> dict:
    keys = jax.random.split(jax.random.key(seed), 8)
    return {
        "element_blocks": draw_element_blocks(jax.random.fold_in(keys[7], 71), 0),
        "mortar_projection": draw_mortar_projection(jax.random.fold_in(keys[7], 71), 0),
        "face_sources": centred(keys[2], (NXE, NYE, 3, FUNC * FD), 1.0, 6.0, ((0, 16), (1, 8)), jnp.float32),
        "coarse_sources": centred(keys[3], (COARSE, N_GY, FUNC * FD), 1.0, 6.0, ((0, 16), (1, 8)), jnp.float32),
        "parent_slot": draw_parent_slot(jax.random.fold_in(keys[7], 71), 0),
        "child_position": draw_child_position(jax.random.fold_in(keys[7], 71), 0),
        "live_count": draw_live_count(jax.random.fold_in(keys[7], 71), 0),
    }


def row_product(operands):
    row_input, row_blocks = operands
    return jnp.einsum("jfa,jab->jfb", row_input.astype(jnp.float32), row_blocks.astype(jnp.float32))


def reference(element_blocks, mortar_projection, face_sources, coarse_sources, parent_slot, child_position, live_count):
    highest = lax.Precision.HIGHEST
    row_index = lax.broadcasted_iota(jnp.int32, (NXE, NYE), 0)
    col_index = lax.broadcasted_iota(jnp.int32, (NXE, NYE), 1)
    column = (col_index // ELY).astype(jnp.int32)
    local_index = (row_index % ELX) * ELY + col_index % ELY
    live = (local_index < live_count[row_index // ELX, column]).astype(jnp.float32)
    chosen = mortar_projection[child_position]
    sources = face_sources.reshape(NXE, NYE, 3, FUNC, FD)
    coarse_src = coarse_sources.reshape(COARSE, N_GY, FUNC, FD)
    face_state = jnp.zeros((NXE, NYE, 3, FUNC, FD), jnp.float32)
    coarse_state = jnp.zeros((COARSE, N_GY, FUNC, FD), jnp.float32)
    for sweep_index in range(ITERS):
        east_face = face_state[:, :, 0]
        north_face = face_state[:, :, 1]
        bottom_face = face_state[:, :, 2]
        west_face = jnp.roll(east_face, 1, 0)
        south_face = jnp.roll(north_face, 1, 1)
        above = coarse_state[parent_slot, column]
        top_face = jnp.einsum("ijfk,ijlk->ijfl", above, chosen, precision=highest)
        local_in = jnp.concatenate([west_face, east_face, south_face, north_face, bottom_face, top_face], -1).astype(jnp.bfloat16)
        contrib = lax.map(row_product, (local_in, element_blocks))
        contrib = contrib * live[:, :, None, None]
        west_part = contrib[..., 0:FD]
        east_part = contrib[..., FD:2 * FD]
        south_part = contrib[..., 2 * FD:3 * FD]
        north_part = contrib[..., 3 * FD:4 * FD]
        bottom_part = contrib[..., 4 * FD:5 * FD]
        top_part = contrib[..., 5 * FD:6 * FD]
        east_sum = east_part + jnp.roll(west_part, -1, 0)
        north_sum = north_part + jnp.roll(south_part, -1, 1)
        face_sum = jnp.stack([east_sum, north_sum, bottom_part], 2)
        projected = jnp.einsum("ijfl,ijlk->ijfk", top_part, chosen, precision=highest)
        coarse_sum = jnp.zeros((COARSE, N_GY, FUNC, FD), jnp.float32).at[parent_slot, column].add(projected)
        face_state = face_state + 0.8 * (sources - face_sum)
        coarse_state = coarse_state + 0.8 * (coarse_src - coarse_sum)
    return face_state.reshape(NXE, NYE, 3, FUNC * FD), coarse_state.reshape(COARSE, N_GY, FUNC * FD)
```

```python
import jax
import jax.numpy as jnp
from jax import lax
from jax.sharding import PartitionSpec as P

ITERS = 4


OMEGA = 0.8


def extended(cells, sides, width):
    for axis, dim in sides:
        count = lax.axis_size(axis)
        head = lax.slice_in_dim(cells, 0, width, axis=dim)
        tail = lax.slice_in_dim(cells, cells.shape[dim] - width, cells.shape[dim], axis=dim)
        cells = jnp.concatenate(
            [
                lax.ppermute(tail, axis, [(i, (i + 1) % count) for i in range(count)]),
                cells,
                lax.ppermute(head, axis, [((i + 1) % count, i) for i in range(count)]),
            ],
            axis=dim,
        )
    return cells


def rims_along_first(block):
    return extended(block, (("gx", 0),), 1)


def rims_along_second(block):
    return extended(block, (("gy", 1),), 1)


def shards(
    element_blocks,
    mortar_projection,
    face_sources,
    coarse_sources,
    parent_slot,
    child_position,
    live_count,
):
    highest = lax.Precision.HIGHEST
    tile_rows, tile_cols = parent_slot.shape
    trace_width = face_sources.shape[-1]
    face_dofs = mortar_projection.shape[-1]
    functionals = trace_width // face_dofs
    sources = lax.axis_size("gx")
    owner_slots = coarse_sources.shape[0]
    per_pair = owner_slots // sources
    element_count = tile_rows * tile_cols
    send_slots = sources * per_pair
    block_width = element_blocks.shape[-1]
    row_index = lax.broadcasted_iota(jnp.int32, (tile_rows, tile_cols), 0)
    col_index = lax.broadcasted_iota(jnp.int32, (tile_rows, tile_cols), 1)
    live_mask = (row_index * tile_cols + col_index < live_count[0, 0]).astype(jnp.float32)
    live_flat = live_mask.reshape(element_count)
    parents = parent_slot.reshape(element_count)
    positions = child_position.reshape(element_count)
    targets = (
        parents // owner_slots * per_pair + parents % owner_slots - lax.axis_index("gx") * per_pair
    )
    routing = (targets[None, :] == jnp.arange(send_slots, dtype=jnp.int32)[:, None]).astype(
        jnp.float32
    )
    position_hot = (positions[:, None] == jnp.arange(4, dtype=jnp.int32)[None, :]).astype(
        jnp.float32
    )
    chosen = jnp.einsum("ek,kab->eab", position_hot, mortar_projection, precision=highest)
    blocks = element_blocks.reshape(element_count, block_width, block_width)
    face_src = face_sources.reshape(tile_rows, tile_cols, 3, functionals, face_dofs)
    coarse_source = lax.all_to_all(
        coarse_sources[:, 0, :].reshape(sources, per_pair, functionals, face_dofs),
        "gx",
        split_axis=0,
        concat_axis=0,
        tiled=True,
    ).reshape(send_slots, functionals, face_dofs)
    west_source = rims_along_first(face_src[-1:, :, 0])[0]
    south_source = rims_along_second(face_src[:, -1:, 1])[:, 0]
    face_state = OMEGA * face_src
    west_ghost = OMEGA * west_source
    south_ghost = OMEGA * south_source
    coarse_state = OMEGA * coarse_source
    for sweep_index in range(1, ITERS):
        east_face = face_state[:, :, 0]
        north_face = face_state[:, :, 1]
        bottom_face = face_state[:, :, 2]
        west_face = jnp.concatenate([west_ghost[None], east_face[:-1]], 0)
        south_face = jnp.concatenate([south_ghost[:, None], north_face[:, :-1]], 1)
        coarse_here = jnp.einsum("se,sfk->efk", routing, coarse_state, precision=highest)
        top_face = jnp.einsum("efk,elk->efl", coarse_here, chosen, precision=highest).reshape(
            tile_rows, tile_cols, functionals, face_dofs
        )
        local_in = jnp.concatenate(
            [west_face, east_face, south_face, north_face, bottom_face, top_face], -1
        ).astype(jnp.bfloat16)
        result = jnp.einsum(
            "efa,eac->efc",
            local_in.reshape(element_count, functionals, block_width),
            blocks,
            preferred_element_type=jnp.float32,
        )
        result = result * live_flat[:, None, None]
        result = result.reshape(tile_rows, tile_cols, functionals, 6, face_dofs)
        west_part = result[:, :, :, 0]
        east_part = result[:, :, :, 1]
        south_part = result[:, :, :, 2]
        north_part = result[:, :, :, 3]
        bottom_part = result[:, :, :, 4]
        top_part = result[:, :, :, 5]
        first_rim = rims_along_first(jnp.stack([west_part[0], east_part[-1]], 0))
        second_rim = rims_along_second(jnp.stack([south_part[:, 0], north_part[:, -1]], 1))
        east_sum = east_part + jnp.concatenate([west_part[1:], first_rim[3][None]], 0)
        north_sum = north_part + jnp.concatenate([south_part[:, 1:], second_rim[:, 3][:, None]], 1)
        west_sum = first_rim[0] + west_part[0]
        south_sum = second_rim[:, 0] + south_part[:, 0]
        top_flat = top_part.reshape(element_count, functionals, face_dofs)
        projected = jnp.einsum("efl,elk->efk", top_flat, chosen, precision=highest)
        coarse_sum = jnp.einsum("se,efk->sfk", routing, projected, precision=highest)
        face_sum = jnp.stack([east_sum, north_sum, bottom_part], 2)
        face_state = face_state + OMEGA * (face_src - face_sum)
        west_ghost = west_ghost + OMEGA * (west_source - west_sum)
        south_ghost = south_ghost + OMEGA * (south_source - south_sum)
        coarse_state = coarse_state + OMEGA * (coarse_source - coarse_sum)
    coarse_out = lax.all_to_all(
        coarse_state.reshape(sources, per_pair, functionals, face_dofs),
        "gx",
        split_axis=0,
        concat_axis=0,
        tiled=True,
    )
    face_out = face_state.reshape(tile_rows, tile_cols, 3, trace_width)
    coarse_out = coarse_out.reshape(owner_slots, 1, trace_width)
    return (face_out, coarse_out)


def solution(mesh):
    return jax.shard_map(
        shards,
        mesh=mesh,
        in_specs=(
            P("gx", "gy", None, None),
            P(),
            P("gx", "gy", None, None),
            P("gx", "gy", None),
            P("gx", "gy"),
            P("gx", "gy"),
            P("gx", "gy"),
        ),
        out_specs=(P("gx", "gy", None, None), P("gx", "gy", None)),
        check_vma=False,
    )
```

```python
import jax
import jax.numpy as jnp
from jax import lax
from jax.sharding import PartitionSpec as P

ITERS = 4


OMEGA = 0.8


def extended(cells, sides, width):
    for axis, dim in sides:
        count = lax.axis_size(axis)
        head = lax.slice_in_dim(cells, 0, width, axis=dim)
        tail = lax.slice_in_dim(cells, cells.shape[dim] - width, cells.shape[dim], axis=dim)
        cells = jnp.concatenate(
            [
                lax.ppermute(tail, axis, [(i, (i + 1) % count) for i in range(count)]),
                cells,
                lax.ppermute(head, axis, [((i + 1) % count, i) for i in range(count)]),
            ],
            axis=dim,
        )
    return cells


def rims_along_first(block):
    return extended(block, (("gx", 0),), 1)


def rims_along_second(block):
    return extended(block, (("gy", 1),), 1)


def shards(
    element_blocks,
    mortar_projection,
    face_sources,
    coarse_sources,
    parent_slot,
    child_position,
    live_count,
):
    highest = lax.Precision.HIGHEST
    tile_rows, tile_cols = parent_slot.shape
    trace_width = face_sources.shape[-1]
    face_dofs = mortar_projection.shape[-1]
    functionals = trace_width // face_dofs
    sources = lax.axis_size("gx")
    owner_slots = coarse_sources.shape[0]
    per_pair = owner_slots // sources
    element_count = tile_rows * tile_cols
    send_slots = sources * per_pair
    block_width = element_blocks.shape[-1]
    row_index = lax.broadcasted_iota(jnp.int32, (tile_rows, tile_cols), 0)
    col_index = lax.broadcasted_iota(jnp.int32, (tile_rows, tile_cols), 1)
    live_mask = (row_index * tile_cols + col_index < live_count[0, 0]).astype(jnp.float32)
    live_flat = live_mask.reshape(element_count)
    parents = parent_slot.reshape(element_count)
    positions = child_position.reshape(element_count)
    targets = (
        parents // owner_slots * per_pair + parents % owner_slots - lax.axis_index("gx") * per_pair
    )
    combos = 4 * send_slots
    pair_index = positions * send_slots + targets
    pair_match = pair_index[None, :] == jnp.arange(combos, dtype=jnp.int32)[:, None]
    pair_owner = jnp.sum(
        jnp.where(pair_match, jnp.arange(element_count, dtype=jnp.int32)[None, :], 0), 1
    ) + jnp.where(jnp.any(pair_match, 1), 0, element_count)
    blocks = element_blocks.reshape(element_count, block_width, block_width)
    face_src = face_sources.reshape(tile_rows, tile_cols, 3, functionals, face_dofs)
    coarse_source = lax.all_to_all(
        coarse_sources[:, 0, :].reshape(sources, per_pair, functionals, face_dofs),
        "gx",
        split_axis=0,
        concat_axis=0,
        tiled=True,
    ).reshape(send_slots, functionals, face_dofs)
    west_source = rims_along_first(face_src[-1:, :, 0])[0]
    south_source = rims_along_second(face_src[:, -1:, 1])[:, 0]
    face_state = OMEGA * face_src
    west_ghost = OMEGA * west_source
    south_ghost = OMEGA * south_source
    coarse_state = OMEGA * coarse_source
    def sweep(_, carry):
        face_state, west_ghost, south_ghost, coarse_state = carry
        east_face = face_state[:, :, 0]
        north_face = face_state[:, :, 1]
        bottom_face = face_state[:, :, 2]
        west_face = jnp.concatenate([west_ghost[None], east_face[:-1]], 0)
        south_face = jnp.concatenate([south_ghost[:, None], north_face[:, :-1]], 1)
        every_top = jnp.einsum(
            "tfk,plk->ptfl", coarse_state, mortar_projection, precision=highest
        ).reshape(combos, functionals, face_dofs)
        top_face = jnp.take(every_top, pair_index, axis=0, mode="clip").reshape(
            tile_rows, tile_cols, functionals, face_dofs
        )
        local_in = jnp.concatenate(
            [west_face, east_face, south_face, north_face, bottom_face, top_face], -1
        ).astype(jnp.bfloat16)
        result = jnp.einsum(
            "efa,eac->efc",
            local_in.reshape(element_count, functionals, block_width),
            blocks,
            preferred_element_type=jnp.float32,
        )
        result = result * live_flat[:, None, None]
        result = result.reshape(tile_rows, tile_cols, functionals, 6, face_dofs)
        west_part = result[:, :, :, 0]
        east_part = result[:, :, :, 1]
        south_part = result[:, :, :, 2]
        north_part = result[:, :, :, 3]
        bottom_part = result[:, :, :, 4]
        top_part = result[:, :, :, 5]
        first_rim = rims_along_first(jnp.stack([west_part[0], east_part[-1]], 0))
        second_rim = rims_along_second(jnp.stack([south_part[:, 0], north_part[:, -1]], 1))
        east_sum = east_part + jnp.concatenate([west_part[1:], first_rim[3][None]], 0)
        north_sum = north_part + jnp.concatenate([south_part[:, 1:], second_rim[:, 3][:, None]], 1)
        west_sum = first_rim[0] + west_part[0]
        south_sum = second_rim[:, 0] + south_part[:, 0]
        top_flat = top_part.reshape(element_count, functionals, face_dofs)
        padded_top = jnp.concatenate(
            [top_flat, jnp.zeros((1, functionals, face_dofs), jnp.float32)], 0
        )
        by_pair = jnp.take(padded_top, pair_owner, axis=0, mode="clip").reshape(
            4, send_slots, functionals, face_dofs
        )
        coarse_sum = jnp.einsum("ptfl,plk->tfk", by_pair, mortar_projection, precision=highest)
        face_sum = jnp.stack([east_sum, north_sum, bottom_part], 2)
        face_state = face_state + OMEGA * (face_src - face_sum)
        west_ghost = west_ghost + OMEGA * (west_source - west_sum)
        south_ghost = south_ghost + OMEGA * (south_source - south_sum)
        coarse_state = coarse_state + OMEGA * (coarse_source - coarse_sum)
        return face_state, west_ghost, south_ghost, coarse_state

    face_state, west_ghost, south_ghost, coarse_state = lax.fori_loop(
        1, ITERS, sweep, (face_state, west_ghost, south_ghost, coarse_state)
    )
    coarse_out = lax.all_to_all(
        coarse_state.reshape(sources, per_pair, functionals, face_dofs),
        "gx",
        split_axis=0,
        concat_axis=0,
        tiled=True,
    )
    face_out = face_state.reshape(tile_rows, tile_cols, 3, trace_width)
    coarse_out = coarse_out.reshape(owner_slots, 1, trace_width)
    return (face_out, coarse_out)


def solution(mesh):
    return jax.shard_map(
        shards,
        mesh=mesh,
        in_specs=(
            P("gx", "gy", None, None),
            P(),
            P("gx", "gy", None, None),
            P("gx", "gy", None),
            P("gx", "gy"),
            P("gx", "gy"),
            P("gx", "gy"),
        ),
        out_specs=(P("gx", "gy", None, None), P("gx", "gy", None)),
        check_vma=False,
    )
```

```python
import jax
import jax.numpy as jnp
from jax import lax
from jax.experimental import pallas as pl
from jax.sharding import PartitionSpec as P

ITERS = 4


OMEGA = 0.8

GROUP = 8


def extended(cells, sides, width):
    for axis, dim in sides:
        count = lax.axis_size(axis)
        head = lax.slice_in_dim(cells, 0, width, axis=dim)
        tail = lax.slice_in_dim(cells, cells.shape[dim] - width, cells.shape[dim], axis=dim)
        cells = jnp.concatenate(
            [
                lax.ppermute(tail, axis, [(i, (i + 1) % count) for i in range(count)]),
                cells,
                lax.ppermute(head, axis, [((i + 1) % count, i) for i in range(count)]),
            ],
            axis=dim,
        )
    return cells


def rims_along_first(block, dim=0):
    return extended(block, (("gx", dim),), 1)


def rims_along_second(block, dim=1):
    return extended(block, (("gy", dim),), 1)


def block_products(pieces, blocks):
    parts, count, functionals, face_dofs = pieces.shape
    width = blocks.shape[-1]
    group = GROUP if count % GROUP == 0 else 1

    def kernel(x_ref, b_ref, o_ref):
        for e in range(group):
            row = jnp.concatenate([x_ref[h, e] for h in range(parts)], axis=-1)
            out = jnp.dot(row.astype(jnp.bfloat16), b_ref[e], preferred_element_type=jnp.float32)
            for g in range(parts):
                o_ref[g, e] = out[:, g * face_dofs : (g + 1) * face_dofs]

    return pl.pallas_call(
        kernel,
        grid=(count // group,),
        in_specs=[
            pl.BlockSpec((parts, group, functionals, face_dofs), lambda i: (0, i, 0, 0)),
            pl.BlockSpec((group, width, width), lambda i: (i, 0, 0)),
        ],
        out_specs=pl.BlockSpec((parts, group, functionals, face_dofs), lambda i: (0, i, 0, 0)),
        out_shape=jax.ShapeDtypeStruct(pieces.shape, jnp.float32),
    )(pieces, blocks)


def shards(
    element_blocks,
    mortar_projection,
    face_sources,
    coarse_sources,
    parent_slot,
    child_position,
    live_count,
):
    highest = lax.Precision.HIGHEST
    tile_rows, tile_cols = parent_slot.shape
    trace_width = face_sources.shape[-1]
    face_dofs = mortar_projection.shape[-1]
    functionals = trace_width // face_dofs
    sources = lax.axis_size("gx")
    owner_slots = coarse_sources.shape[0]
    per_pair = owner_slots // sources
    element_count = tile_rows * tile_cols
    send_slots = sources * per_pair
    block_width = element_blocks.shape[-1]
    row_index = lax.broadcasted_iota(jnp.int32, (tile_rows, tile_cols), 0)
    col_index = lax.broadcasted_iota(jnp.int32, (tile_rows, tile_cols), 1)
    live_mask = (row_index * tile_cols + col_index < live_count[0, 0]).astype(jnp.float32)
    parents = parent_slot.reshape(element_count)
    positions = child_position.reshape(element_count)
    targets = (
        parents // owner_slots * per_pair + parents % owner_slots - lax.axis_index("gx") * per_pair
    )
    combos = 4 * send_slots
    pair_index = positions * send_slots + targets
    pair_match = pair_index[None, :] == jnp.arange(combos, dtype=jnp.int32)[:, None]
    pair_owner = jnp.sum(
        jnp.where(pair_match, jnp.arange(element_count, dtype=jnp.int32)[None, :], 0), 1
    ) + jnp.where(jnp.any(pair_match, 1), 0, element_count)
    blocks = element_blocks.reshape(element_count, block_width, block_width)
    face_src = jnp.moveaxis(
        face_sources.reshape(tile_rows, tile_cols, 3, functionals, face_dofs), 2, 0
    )
    coarse_source = lax.all_to_all(
        coarse_sources[:, 0, :].reshape(sources, per_pair, functionals, face_dofs),
        "gx",
        split_axis=0,
        concat_axis=0,
        tiled=True,
    ).reshape(send_slots, functionals, face_dofs)
    west_source = rims_along_first(face_src[0, -1:], 0)[0]
    south_source = rims_along_second(face_src[1, :, -1:], 1)[:, 0]
    face_state = OMEGA * face_src
    west_ghost = OMEGA * west_source
    south_ghost = OMEGA * south_source
    coarse_state = OMEGA * coarse_source

    def sweep(_, carry):
        face_state, west_ghost, south_ghost, coarse_state = carry
        east_face = face_state[0]
        north_face = face_state[1]
        bottom_face = face_state[2]
        west_face = jnp.concatenate([west_ghost[None], east_face[:-1]], 0)
        south_face = jnp.concatenate([south_ghost[:, None], north_face[:, :-1]], 1)
        every_top = jnp.einsum(
            "tfk,plk->ptfl", coarse_state, mortar_projection, precision=highest
        ).reshape(combos, functionals, face_dofs)
        top_face = jnp.take(every_top, pair_index, axis=0, mode="clip").reshape(
            tile_rows, tile_cols, functionals, face_dofs
        )
        local_in = jnp.stack(
            [west_face, east_face, south_face, north_face, bottom_face, top_face], 0
        ).reshape(6, element_count, functionals, face_dofs)
        result = block_products(local_in, blocks).reshape(
            6, tile_rows, tile_cols, functionals, face_dofs
        )
        result = result * live_mask[None, :, :, None, None]
        west_part = result[0]
        east_part = result[1]
        south_part = result[2]
        north_part = result[3]
        bottom_part = result[4]
        top_part = result[5]
        first_rim = rims_along_first(jnp.stack([west_part[0], east_part[-1]], 0))
        second_rim = rims_along_second(jnp.stack([south_part[:, 0], north_part[:, -1]], 1))
        east_sum = east_part + jnp.concatenate([west_part[1:], first_rim[3][None]], 0)
        north_sum = north_part + jnp.concatenate([south_part[:, 1:], second_rim[:, 3][:, None]], 1)
        west_sum = first_rim[0] + west_part[0]
        south_sum = second_rim[:, 0] + south_part[:, 0]
        top_flat = top_part.reshape(element_count, functionals, face_dofs)
        padded_top = jnp.concatenate(
            [top_flat, jnp.zeros((1, functionals, face_dofs), jnp.float32)], 0
        )
        by_pair = jnp.take(padded_top, pair_owner, axis=0, mode="clip").reshape(
            4, send_slots, functionals, face_dofs
        )
        coarse_sum = jnp.einsum("ptfl,plk->tfk", by_pair, mortar_projection, precision=highest)
        face_sum = jnp.stack([east_sum, north_sum, bottom_part], 0)
        face_state = face_state + OMEGA * (face_src - face_sum)
        west_ghost = west_ghost + OMEGA * (west_source - west_sum)
        south_ghost = south_ghost + OMEGA * (south_source - south_sum)
        coarse_state = coarse_state + OMEGA * (coarse_source - coarse_sum)
        return face_state, west_ghost, south_ghost, coarse_state

    carry = lax.fori_loop(
        1, ITERS - 1, sweep, (face_state, west_ghost, south_ghost, coarse_state)
    )
    face_state, _, _, coarse_state = sweep(ITERS - 1, carry)
    coarse_out = lax.all_to_all(
        coarse_state.reshape(sources, per_pair, functionals, face_dofs),
        "gx",
        split_axis=0,
        concat_axis=0,
        tiled=True,
    )
    face_out = jnp.moveaxis(face_state, 0, 2).reshape(tile_rows, tile_cols, 3, trace_width)
    coarse_out = coarse_out.reshape(owner_slots, 1, trace_width)
    return (face_out, coarse_out)


def solution(mesh):
    return jax.shard_map(
        shards,
        mesh=mesh,
        in_specs=(
            P("gx", "gy", None, None),
            P(),
            P("gx", "gy", None, None),
            P("gx", "gy", None),
            P("gx", "gy"),
            P("gx", "gy"),
            P("gx", "gy"),
        ),
        out_specs=(P("gx", "gy", None, None), P("gx", "gy", None)),
        check_vma=False,
    )
```

```python
import jax
import jax.numpy as jnp
from jax import lax
from jax.experimental import pallas as pl
from jax.experimental.pallas import tpu as pltpu
from jax.sharding import PartitionSpec as P

ITERS = 4


OMEGA = 0.8


def extended(cells, sides, width):
    for axis, dim in sides:
        count = lax.axis_size(axis)
        head = lax.slice_in_dim(cells, 0, width, axis=dim)
        tail = lax.slice_in_dim(cells, cells.shape[dim] - width, cells.shape[dim], axis=dim)
        cells = jnp.concatenate(
            [
                lax.ppermute(tail, axis, [(i, (i + 1) % count) for i in range(count)]),
                cells,
                lax.ppermute(head, axis, [((i + 1) % count, i) for i in range(count)]),
            ],
            axis=dim,
        )
    return cells


def to_next(block, axis):
    count = lax.axis_size(axis)
    return lax.ppermute(block, axis, [(i, (i + 1) % count) for i in range(count)])


def to_previous(block, axis):
    count = lax.axis_size(axis)
    return lax.ppermute(block, axis, [((i + 1) % count, i) for i in range(count)])


def apply_update(fs, src, wg, sg, wsrc, ssrc, prev, from_e, from_w, from_n, from_s, fs_o, wg_o, sg_o):
    rows, cols = fs.shape[1], fs.shape[2]
    for i in range(rows):
        neighbour = prev[0, i + 1] if i + 1 < rows else from_e[...]
        fs_o[0, i] = fs[0, i] + OMEGA * (src[0, i] - (prev[1, i] + neighbour))
    for j in range(cols):
        neighbour = prev[2, :, j + 1] if j + 1 < cols else from_n[...]
        fs_o[1, :, j] = fs[1, :, j] + OMEGA * (src[1, :, j] - (prev[3, :, j] + neighbour))
    fs_o[2] = fs[2] + OMEGA * (src[2] - prev[4])
    wg_o[...] = wg[...] + OMEGA * (wsrc[...] - (from_w[...] + prev[0, 0]))
    sg_o[...] = sg[...] + OMEGA * (ssrc[...] - (from_s[...] + prev[2, :, 0]))


def whole(shape):
    return pl.BlockSpec(shape, lambda *_: (0,) * len(shape))


def sweep_call(count, fs, src, wg, sg, wsrc, ssrc, prev, from_e, from_w, from_n, from_s, top, blocks):
    _, rows, cols, functionals, face_dofs = fs.shape
    width = blocks.shape[-1]

    def kernel(count_ref, fs_r, src_r, wg_r, sg_r, wsrc_r, ssrc_r, prev_r, fe_r, fw_r, fn_r,
               fsr_r, top_r, b_r, fs_o, wg_o, sg_o, c_o, to_w, to_e, to_s, to_n):
        i = pl.program_id(0)

        @pl.when(i == 0)
        def _():
            apply_update(fs_r, src_r, wg_r, sg_r, wsrc_r, ssrc_r, prev_r, fe_r, fw_r, fn_r,
                         fsr_r, fs_o, wg_o, sg_o)

        for j in range(cols):
            west = jnp.where(i == 0, wg_o[j], fs_o[0, jnp.maximum(i - 1, 0), j])
            south = sg_o[i] if j == 0 else fs_o[1, i, j - 1]
            row = jnp.concatenate(
                [west, fs_o[0, i, j], south, fs_o[1, i, j], fs_o[2, i, j], top_r[i, j]], -1
            )
            out = jnp.dot(row.astype(jnp.bfloat16), b_r[0, j], preferred_element_type=jnp.float32)
            live = ((i * cols + j) < count_ref[0]).astype(jnp.float32)
            out = out * live
            for g in range(6):
                c_o[g, i, j] = out[:, g * face_dofs : (g + 1) * face_dofs]
            if j == 0:
                to_s[i] = out[:, 2 * face_dofs : 3 * face_dofs]
            if j == cols - 1:
                to_n[i] = out[:, 3 * face_dofs : 4 * face_dofs]

        @pl.when(i == 0)
        def _():
            to_w[...] = c_o[0, 0]

        @pl.when(i == rows - 1)
        def _():
            to_e[...] = c_o[1, rows - 1]

    f32 = jnp.float32
    operands = (fs, src, wg, sg, wsrc, ssrc, prev, from_e, from_w, from_n, from_s, top)
    out_shape = (
        jax.ShapeDtypeStruct(fs.shape, f32),
        jax.ShapeDtypeStruct(wg.shape, f32),
        jax.ShapeDtypeStruct(sg.shape, f32),
        jax.ShapeDtypeStruct(prev.shape, f32),
        jax.ShapeDtypeStruct(wg.shape, f32),
        jax.ShapeDtypeStruct(wg.shape, f32),
        jax.ShapeDtypeStruct(sg.shape, f32),
        jax.ShapeDtypeStruct(sg.shape, f32),
    )
    grid_spec = pltpu.PrefetchScalarGridSpec(
        num_scalar_prefetch=1,
        grid=(rows,),
        in_specs=[whole(a.shape) for a in operands]
        + [pl.BlockSpec((1, cols, width, width), lambda i, *_: (i, 0, 0, 0))],
        out_specs=[whole(s.shape) for s in out_shape],
    )
    return pl.pallas_call(kernel, grid_spec=grid_spec, out_shape=out_shape)(
        count, *operands, blocks
    )


def final_update(fs, src, wg, sg, wsrc, ssrc, prev, from_e, from_w, from_n, from_s):
    def kernel(fs_r, src_r, wg_r, sg_r, wsrc_r, ssrc_r, prev_r, fe_r, fw_r, fn_r, fsr_r,
               fs_o, wg_o, sg_o):
        apply_update(fs_r, src_r, wg_r, sg_r, wsrc_r, ssrc_r, prev_r, fe_r, fw_r, fn_r, fsr_r,
                     fs_o, wg_o, sg_o)

    f32 = jnp.float32
    out_shape = (
        jax.ShapeDtypeStruct(fs.shape, f32),
        jax.ShapeDtypeStruct(wg.shape, f32),
        jax.ShapeDtypeStruct(sg.shape, f32),
    )
    return pl.pallas_call(kernel, out_shape=out_shape)(
        fs, src, wg, sg, wsrc, ssrc, prev, from_e, from_w, from_n, from_s
    )[0]


def shards(
    element_blocks,
    mortar_projection,
    face_sources,
    coarse_sources,
    parent_slot,
    child_position,
    live_count,
):
    highest = lax.Precision.HIGHEST
    tile_rows, tile_cols = parent_slot.shape
    trace_width = face_sources.shape[-1]
    face_dofs = mortar_projection.shape[-1]
    functionals = trace_width // face_dofs
    sources = lax.axis_size("gx")
    owner_slots = coarse_sources.shape[0]
    per_pair = owner_slots // sources
    element_count = tile_rows * tile_cols
    send_slots = sources * per_pair
    count = live_count.reshape(1)
    parents = parent_slot.reshape(element_count)
    positions = child_position.reshape(element_count)
    targets = (
        parents // owner_slots * per_pair + parents % owner_slots - lax.axis_index("gx") * per_pair
    )
    combos = 4 * send_slots
    pair_index = positions * send_slots + targets
    pair_match = pair_index[None, :] == jnp.arange(combos, dtype=jnp.int32)[:, None]
    pair_owner = jnp.sum(
        jnp.where(pair_match, jnp.arange(element_count, dtype=jnp.int32)[None, :], 0), 1
    ) + jnp.where(jnp.any(pair_match, 1), 0, element_count)
    face_src = jnp.moveaxis(
        face_sources.reshape(tile_rows, tile_cols, 3, functionals, face_dofs), 2, 0
    )
    coarse_source = lax.all_to_all(
        coarse_sources[:, 0, :].reshape(sources, per_pair, functionals, face_dofs),
        "gx",
        split_axis=0,
        concat_axis=0,
        tiled=True,
    ).reshape(send_slots, functionals, face_dofs)
    west_source = extended(face_src[0, -1:], (("gx", 0),), 1)[0]
    south_source = extended(face_src[1, :, -1:], (("gy", 1),), 1)[:, 0]

    def coarse_update(coarse_state, prev):
        top_flat = prev[5].reshape(element_count, functionals, face_dofs)
        padded_top = jnp.concatenate(
            [top_flat, jnp.zeros((1, functionals, face_dofs), jnp.float32)], 0
        )
        by_pair = jnp.take(padded_top, pair_owner, axis=0, mode="clip").reshape(
            4, send_slots, functionals, face_dofs
        )
        coarse_sum = jnp.einsum("ptfl,plk->tfk", by_pair, mortar_projection, precision=highest)
        return coarse_state + OMEGA * (coarse_source - coarse_sum)

    def sweep(_, carry):
        face_state, west_ghost, south_ghost, coarse_state, prev, from_e, from_w, from_n, from_s = carry
        coarse_state = coarse_update(coarse_state, prev)
        every_top = jnp.einsum(
            "tfk,plk->ptfl", coarse_state, mortar_projection, precision=highest
        ).reshape(combos, functionals, face_dofs)
        top_face = jnp.take(every_top, pair_index, axis=0, mode="clip").reshape(
            tile_rows, tile_cols, functionals, face_dofs
        )
        face_state, west_ghost, south_ghost, prev, to_w, to_e, to_s, to_n = sweep_call(
            count, face_state, face_src, west_ghost, south_ghost, west_source, south_source,
            prev, from_e, from_w, from_n, from_s, top_face, element_blocks,
        )
        from_e = to_previous(to_w, "gx")
        from_w = to_next(to_e, "gx")
        from_n = to_previous(to_s, "gy")
        from_s = to_next(to_n, "gy")
        return face_state, west_ghost, south_ghost, coarse_state, prev, from_e, from_w, from_n, from_s

    zeros = jnp.zeros_like
    carry = (
        zeros(face_src),
        zeros(west_source),
        zeros(south_source),
        zeros(coarse_source),
        jnp.zeros((6, tile_rows, tile_cols, functionals, face_dofs), jnp.float32),
        zeros(west_source),
        zeros(west_source),
        zeros(south_source),
        zeros(south_source),
    )
    carry = lax.fori_loop(1, ITERS, sweep, carry)
    face_state, west_ghost, south_ghost, coarse_state, prev, from_e, from_w, from_n, from_s = carry
    coarse_state = coarse_update(coarse_state, prev)
    coarse_out = lax.all_to_all(
        coarse_state.reshape(sources, per_pair, functionals, face_dofs),
        "gx",
        split_axis=0,
        concat_axis=0,
        tiled=True,
    )
    face_state = final_update(
        face_state, face_src, west_ghost, south_ghost, west_source, south_source,
        prev, from_e, from_w, from_n, from_s,
    )
    face_out = jnp.moveaxis(face_state, 0, 2).reshape(tile_rows, tile_cols, 3, trace_width)
    coarse_out = coarse_out.reshape(owner_slots, 1, trace_width)
    return (face_out, coarse_out)


def solution(mesh):
    return jax.shard_map(
        shards,
        mesh=mesh,
        in_specs=(
            P("gx", "gy", None, None),
            P(),
            P("gx", "gy", None, None),
            P("gx", "gy", None),
            P("gx", "gy"),
            P("gx", "gy"),
            P("gx", "gy"),
        ),
        out_specs=(P("gx", "gy", None, None), P("gx", "gy", None)),
        check_vma=False,
    )
```

```python
import jax
import jax.numpy as jnp
from jax import lax
from jax.experimental import pallas as pl
from jax.experimental.pallas import tpu as pltpu
from jax.sharding import PartitionSpec as P

ITERS = 4


OMEGA = 0.8


def extended(cells, sides, width):
    for axis, dim in sides:
        count = lax.axis_size(axis)
        head = lax.slice_in_dim(cells, 0, width, axis=dim)
        tail = lax.slice_in_dim(cells, cells.shape[dim] - width, cells.shape[dim], axis=dim)
        cells = jnp.concatenate(
            [
                lax.ppermute(tail, axis, [(i, (i + 1) % count) for i in range(count)]),
                cells,
                lax.ppermute(head, axis, [((i + 1) % count, i) for i in range(count)]),
            ],
            axis=dim,
        )
    return cells


def to_next(block, axis):
    count = lax.axis_size(axis)
    return lax.ppermute(block, axis, [(i, (i + 1) % count) for i in range(count)])


def to_previous(block, axis):
    count = lax.axis_size(axis)
    return lax.ppermute(block, axis, [((i + 1) % count, i) for i in range(count)])


def apply_update(fs, src, wg, sg, wsrc, ssrc, prev, from_e, from_w, from_n, from_s, fs_o, wg_o, sg_o):
    rows, cols = fs.shape[1], fs.shape[2]
    for i in range(rows):
        neighbour = prev[0, i + 1] if i + 1 < rows else from_e[...]
        fs_o[0, i] = fs[0, i] + OMEGA * (src[0, i] - (prev[1, i] + neighbour))
    for j in range(cols):
        neighbour = prev[2, :, j + 1] if j + 1 < cols else from_n[...]
        fs_o[1, :, j] = fs[1, :, j] + OMEGA * (src[1, :, j] - (prev[3, :, j] + neighbour))
    fs_o[2] = fs[2] + OMEGA * (src[2] - prev[4])
    wg_o[...] = wg[...] + OMEGA * (wsrc[...] - (from_w[...] + prev[0, 0]))
    sg_o[...] = sg[...] + OMEGA * (ssrc[...] - (from_s[...] + prev[2, :, 0]))


def whole(shape):
    return pl.BlockSpec(shape, lambda *_: (0,) * len(shape))


def sweep_call(count, state, src, wsrc, ssrc, top, blocks):
    _, rows, cols, functionals, face_dofs = src.shape
    width = blocks.shape[-1]

    def kernel(count_ref, *refs):
        if state is None:
            src_r, wsrc_r, ssrc_r, top_r, b_r = refs[:5]
        else:
            fs_r, wg_r, sg_r, prev_r, fe_r, fw_r, fn_r, fsr_r = refs[:8]
            src_r, wsrc_r, ssrc_r, top_r, b_r = refs[8:13]
        fs_o, wg_o, sg_o, c_o, to_w, to_e, to_s, to_n = refs[-8:]
        i = pl.program_id(0)

        @pl.when(i == 0)
        def _():
            if state is None:
                fs_o[...] = OMEGA * src_r[...]
                wg_o[...] = OMEGA * wsrc_r[...]
                sg_o[...] = OMEGA * ssrc_r[...]
            else:
                apply_update(fs_r, src_r, wg_r, sg_r, wsrc_r, ssrc_r, prev_r, fe_r, fw_r, fn_r,
                             fsr_r, fs_o, wg_o, sg_o)

        for j in range(cols):
            west = jnp.where(i == 0, wg_o[j], fs_o[0, jnp.maximum(i - 1, 0), j])
            south = sg_o[i] if j == 0 else fs_o[1, i, j - 1]
            row = jnp.concatenate(
                [west, fs_o[0, i, j], south, fs_o[1, i, j], fs_o[2, i, j], top_r[i, j]], -1
            )
            out = jnp.dot(row.astype(jnp.bfloat16), b_r[0, j], preferred_element_type=jnp.float32)
            live = ((i * cols + j) < count_ref[0]).astype(jnp.float32)
            out = out * live
            for g in range(6):
                c_o[g, i, j] = out[:, g * face_dofs : (g + 1) * face_dofs]
            if j == 0:
                to_s[i] = out[:, 2 * face_dofs : 3 * face_dofs]
            if j == cols - 1:
                to_n[i] = out[:, 3 * face_dofs : 4 * face_dofs]

        @pl.when(i == 0)
        def _():
            to_w[...] = c_o[0, 0]

        @pl.when(i == rows - 1)
        def _():
            to_e[...] = c_o[1, rows - 1]

    f32 = jnp.float32
    operands = (() if state is None else tuple(state)) + (src, wsrc, ssrc, top)
    out_shape = (
        jax.ShapeDtypeStruct(src.shape, f32),
        jax.ShapeDtypeStruct(wsrc.shape, f32),
        jax.ShapeDtypeStruct(ssrc.shape, f32),
        jax.ShapeDtypeStruct((6,) + src.shape[1:], f32),
        jax.ShapeDtypeStruct(wsrc.shape, f32),
        jax.ShapeDtypeStruct(wsrc.shape, f32),
        jax.ShapeDtypeStruct(ssrc.shape, f32),
        jax.ShapeDtypeStruct(ssrc.shape, f32),
    )
    grid_spec = pltpu.PrefetchScalarGridSpec(
        num_scalar_prefetch=1,
        grid=(rows,),
        in_specs=[whole(a.shape) for a in operands]
        + [pl.BlockSpec((1, cols, width, width), lambda i, *_: (i, 0, 0, 0))],
        out_specs=[whole(s.shape) for s in out_shape],
    )
    return pl.pallas_call(kernel, grid_spec=grid_spec, out_shape=out_shape)(
        count, *operands, blocks
    )


def final_update(fs, src, wg, sg, wsrc, ssrc, prev, from_e, from_w, from_n, from_s):
    def kernel(fs_r, src_r, wg_r, sg_r, wsrc_r, ssrc_r, prev_r, fe_r, fw_r, fn_r, fsr_r,
               fs_o, wg_o, sg_o):
        apply_update(fs_r, src_r, wg_r, sg_r, wsrc_r, ssrc_r, prev_r, fe_r, fw_r, fn_r, fsr_r,
                     fs_o, wg_o, sg_o)

    f32 = jnp.float32
    out_shape = (
        jax.ShapeDtypeStruct(fs.shape, f32),
        jax.ShapeDtypeStruct(wg.shape, f32),
        jax.ShapeDtypeStruct(sg.shape, f32),
    )
    return pl.pallas_call(kernel, out_shape=out_shape)(
        fs, src, wg, sg, wsrc, ssrc, prev, from_e, from_w, from_n, from_s
    )[0]


def shards(
    element_blocks,
    mortar_projection,
    face_sources,
    coarse_sources,
    parent_slot,
    child_position,
    live_count,
):
    highest = lax.Precision.HIGHEST
    tile_rows, tile_cols = parent_slot.shape
    trace_width = face_sources.shape[-1]
    face_dofs = mortar_projection.shape[-1]
    functionals = trace_width // face_dofs
    sources = lax.axis_size("gx")
    owner_slots = coarse_sources.shape[0]
    per_pair = owner_slots // sources
    element_count = tile_rows * tile_cols
    send_slots = sources * per_pair
    count = live_count.reshape(1)
    parents = parent_slot.reshape(element_count)
    positions = child_position.reshape(element_count)
    targets = (
        parents // owner_slots * per_pair + parents % owner_slots - lax.axis_index("gx") * per_pair
    )
    combos = 4 * send_slots
    pair_index = positions * send_slots + targets
    pair_match = pair_index[None, :] == jnp.arange(combos, dtype=jnp.int32)[:, None]
    pair_owner = jnp.sum(
        jnp.where(pair_match, jnp.arange(element_count, dtype=jnp.int32)[None, :], 0), 1
    ) + jnp.where(jnp.any(pair_match, 1), 0, element_count)
    face_src = jnp.moveaxis(
        face_sources.reshape(tile_rows, tile_cols, 3, functionals, face_dofs), 2, 0
    )
    coarse_source = lax.all_to_all(
        coarse_sources[:, 0, :].reshape(sources, per_pair, functionals, face_dofs),
        "gx",
        split_axis=0,
        concat_axis=0,
        tiled=True,
    ).reshape(send_slots, functionals, face_dofs)
    west_source = extended(face_src[0, -1:], (("gx", 0),), 1)[0]
    south_source = extended(face_src[1, :, -1:], (("gy", 1),), 1)[:, 0]

    def coarse_update(coarse_state, prev):
        top_flat = prev[5].reshape(element_count, functionals, face_dofs)
        padded_top = jnp.concatenate(
            [top_flat, jnp.zeros((1, functionals, face_dofs), jnp.float32)], 0
        )
        by_pair = jnp.take(padded_top, pair_owner, axis=0, mode="clip").reshape(
            4, send_slots, functionals, face_dofs
        )
        coarse_sum = jnp.einsum("ptfl,plk->tfk", by_pair, mortar_projection, precision=highest)
        return coarse_state + OMEGA * (coarse_source - coarse_sum)

    state = None
    coarse_state = OMEGA * coarse_source
    for sweep_index in range(1, ITERS):
        if state is not None:
            coarse_state = coarse_update(coarse_state, state[3])
        every_top = jnp.einsum(
            "tfk,plk->ptfl", coarse_state, mortar_projection, precision=highest
        ).reshape(combos, functionals, face_dofs)
        top_face = jnp.take(every_top, pair_index, axis=0, mode="clip").reshape(
            tile_rows, tile_cols, functionals, face_dofs
        )
        face_state, west_ghost, south_ghost, prev, to_w, to_e, to_s, to_n = sweep_call(
            count, state, face_src, west_source, south_source, top_face, element_blocks
        )
        state = (
            face_state,
            west_ghost,
            south_ghost,
            prev,
            to_previous(to_w, "gx"),
            to_next(to_e, "gx"),
            to_previous(to_s, "gy"),
            to_next(to_n, "gy"),
        )
    coarse_state = coarse_update(coarse_state, state[3])
    coarse_out = lax.all_to_all(
        coarse_state.reshape(sources, per_pair, functionals, face_dofs),
        "gx",
        split_axis=0,
        concat_axis=0,
        tiled=True,
    )
    face_state, west_ghost, south_ghost, prev, from_e, from_w, from_n, from_s = state
    face_state = final_update(
        face_state, face_src, west_ghost, south_ghost, west_source, south_source,
        prev, from_e, from_w, from_n, from_s,
    )
    face_out = jnp.moveaxis(face_state, 0, 2).reshape(tile_rows, tile_cols, 3, trace_width)
    coarse_out = coarse_out.reshape(owner_slots, 1, trace_width)
    return (face_out, coarse_out)


def solution(mesh):
    return jax.shard_map(
        shards,
        mesh=mesh,
        in_specs=(
            P("gx", "gy", None, None),
            P(),
            P("gx", "gy", None, None),
            P("gx", "gy", None),
            P("gx", "gy"),
            P("gx", "gy"),
            P("gx", "gy"),
        ),
        out_specs=(P("gx", "gy", None, None), P("gx", "gy", None)),
        check_vma=False,
    )
```

```python
import jax
import jax.numpy as jnp
from jax import lax
from jax.experimental import pallas as pl
from jax.experimental.pallas import tpu as pltpu
from jax.sharding import PartitionSpec as P

ITERS = 4


OMEGA = 0.8


def extended(cells, sides, width):
    for axis, dim in sides:
        count = lax.axis_size(axis)
        head = lax.slice_in_dim(cells, 0, width, axis=dim)
        tail = lax.slice_in_dim(cells, cells.shape[dim] - width, cells.shape[dim], axis=dim)
        cells = jnp.concatenate(
            [
                lax.ppermute(tail, axis, [(i, (i + 1) % count) for i in range(count)]),
                cells,
                lax.ppermute(head, axis, [((i + 1) % count, i) for i in range(count)]),
            ],
            axis=dim,
        )
    return cells


def to_next(block, axis):
    count = lax.axis_size(axis)
    return lax.ppermute(block, axis, [(i, (i + 1) % count) for i in range(count)])


def to_previous(block, axis):
    count = lax.axis_size(axis)
    return lax.ppermute(block, axis, [((i + 1) % count, i) for i in range(count)])


def update_row(i, rows, cols, fs, src, prev, prev_next, from_e, from_n, fs_o):
    neighbour = jnp.where(i == rows - 1, from_e[...], prev_next[0, 0])
    fs_o[0, 0] = fs[0, 0] + OMEGA * (src[0, 0] - (prev[1, 0] + neighbour))
    for j in range(cols):
        neighbour = prev[2, 0, j + 1] if j + 1 < cols else from_n[i]
        fs_o[1, 0, j] = fs[1, 0, j] + OMEGA * (src[1, 0, j] - (prev[3, 0, j] + neighbour))
    fs_o[2, 0] = fs[2, 0] + OMEGA * (src[2, 0] - prev[4, 0])


def whole(shape):
    return pl.BlockSpec(shape, lambda *_: (0,) * len(shape))


def by_row(shape):
    block = (shape[0], 1) + tuple(shape[2:])
    return pl.BlockSpec(block, lambda i, *_: (0, i) + (0,) * (len(shape) - 2))


def sweep_call(count, state, src, wsrc, ssrc, top, blocks):
    _, rows, cols, functionals, face_dofs = src.shape
    width = blocks.shape[-1]
    prev_shape = (6,) + src.shape[1:]

    def kernel(count_ref, *refs):
        if state is None:
            src_r, wsrc_r, ssrc_r, top_r, b_r = refs[:5]
        else:
            fs_r, wg_r, sg_r, prev_r, prevn_r, fe_r, fw_r, fn_r, fsr_r = refs[:9]
            src_r, wsrc_r, ssrc_r, top_r, b_r = refs[9:14]
        fs_o, wg_o, sg_o, c_o, to_w, to_e, to_s, to_n, east_above = refs[-9:]
        i = pl.program_id(0)

        if state is None:
            fs_o[...] = OMEGA * src_r[...]

            @pl.when(i == 0)
            def _():
                wg_o[...] = OMEGA * wsrc_r[...]

            sg_o[i] = OMEGA * ssrc_r[i]
        else:
            update_row(i, rows, cols, fs_r, src_r, prev_r, prevn_r, fe_r, fn_r, fs_o)

            @pl.when(i == 0)
            def _():
                wg_o[...] = wg_r[...] + OMEGA * (wsrc_r[...] - (fw_r[...] + prev_r[0, 0]))

            sg_o[i] = sg_r[i] + OMEGA * (ssrc_r[i] - (fsr_r[i] + prev_r[2, 0, 0]))

        west_row = jnp.where(i == 0, wg_o[...], east_above[...])
        for j in range(cols):
            south = sg_o[i] if j == 0 else fs_o[1, 0, j - 1]
            row = jnp.concatenate(
                [west_row[j], fs_o[0, 0, j], south, fs_o[1, 0, j], fs_o[2, 0, j], top_r[0, j]], -1
            )
            out = jnp.dot(row.astype(jnp.bfloat16), b_r[0, j], preferred_element_type=jnp.float32)
            live = ((i * cols + j) < count_ref[0]).astype(jnp.float32)
            out = out * live
            for g in range(6):
                c_o[g, 0, j] = out[:, g * face_dofs : (g + 1) * face_dofs]
            if j == 0:
                to_s[i] = out[:, 2 * face_dofs : 3 * face_dofs]
            if j == cols - 1:
                to_n[i] = out[:, 3 * face_dofs : 4 * face_dofs]

            @pl.when(i == 0)
            def _():
                to_w[j] = out[:, 0:face_dofs]

            @pl.when(i == rows - 1)
            def _():
                to_e[j] = out[:, face_dofs : 2 * face_dofs]

        east_above[...] = fs_o[0, 0]

    f32 = jnp.float32
    tail = (src, wsrc, ssrc, top)
    tail_specs = [
        by_row(src.shape),
        whole(wsrc.shape),
        whole(ssrc.shape),
        pl.BlockSpec((1,) + top.shape[1:], lambda i, *_: (i, 0, 0, 0)),
    ]
    if state is None:
        operands, specs = tail, tail_specs
    else:
        fs, wg, sg, prev, from_e, from_w, from_n, from_s = state
        operands = (fs, wg, sg, prev, prev, from_e, from_w, from_n, from_s) + tail
        specs = [
            by_row(fs.shape),
            whole(wg.shape),
            whole(sg.shape),
            by_row(prev.shape),
            pl.BlockSpec(
                (1, 1) + prev.shape[2:],
                lambda i, *_: (0, jnp.minimum(i + 1, rows - 1), 0, 0, 0),
            ),
            whole(from_e.shape),
            whole(from_w.shape),
            whole(from_n.shape),
            whole(from_s.shape),
        ] + tail_specs
    out_shape = (
        jax.ShapeDtypeStruct(src.shape, f32),
        jax.ShapeDtypeStruct(wsrc.shape, f32),
        jax.ShapeDtypeStruct(ssrc.shape, f32),
        jax.ShapeDtypeStruct(prev_shape, f32),
        jax.ShapeDtypeStruct(wsrc.shape, f32),
        jax.ShapeDtypeStruct(wsrc.shape, f32),
        jax.ShapeDtypeStruct(ssrc.shape, f32),
        jax.ShapeDtypeStruct(ssrc.shape, f32),
    )
    out_specs = [by_row(src.shape)] + [whole(wsrc.shape), whole(ssrc.shape)]
    out_specs += [by_row(prev_shape)] + [whole(s.shape) for s in out_shape[4:]]
    grid_spec = pltpu.PrefetchScalarGridSpec(
        num_scalar_prefetch=1,
        grid=(rows,),
        in_specs=specs + [pl.BlockSpec((1, cols, width, width), lambda i, *_: (i, 0, 0, 0))],
        out_specs=out_specs,
        scratch_shapes=[pltpu.VMEM(wsrc.shape, f32)],
    )
    return pl.pallas_call(kernel, grid_spec=grid_spec, out_shape=out_shape)(
        count, *operands, blocks
    )


def final_update(fs, src, prev, from_e, from_n):
    _, rows, cols, functionals, face_dofs = fs.shape

    def kernel(fs_r, src_r, prev_r, prevn_r, fe_r, fn_r, fs_o):
        update_row(pl.program_id(0), rows, cols, fs_r, src_r, prev_r, prevn_r, fe_r, fn_r, fs_o)

    return pl.pallas_call(
        kernel,
        grid=(rows,),
        in_specs=[
            by_row(fs.shape),
            by_row(src.shape),
            pl.BlockSpec((5, 1) + prev.shape[2:], lambda i: (0, i, 0, 0, 0)),
            pl.BlockSpec(
                (1, 1) + prev.shape[2:], lambda i: (0, jnp.minimum(i + 1, rows - 1), 0, 0, 0)
            ),
            whole(from_e.shape),
            whole(from_n.shape),
        ],
        out_specs=by_row(fs.shape),
        out_shape=jax.ShapeDtypeStruct(fs.shape, jnp.float32),
    )(fs, src, prev, prev, from_e, from_n)


def shards(
    element_blocks,
    mortar_projection,
    face_sources,
    coarse_sources,
    parent_slot,
    child_position,
    live_count,
):
    highest = lax.Precision.HIGHEST
    tile_rows, tile_cols = parent_slot.shape
    trace_width = face_sources.shape[-1]
    face_dofs = mortar_projection.shape[-1]
    functionals = trace_width // face_dofs
    sources = lax.axis_size("gx")
    owner_slots = coarse_sources.shape[0]
    per_pair = owner_slots // sources
    element_count = tile_rows * tile_cols
    send_slots = sources * per_pair
    count = live_count.reshape(1)
    parents = parent_slot.reshape(element_count)
    positions = child_position.reshape(element_count)
    targets = (
        parents // owner_slots * per_pair + parents % owner_slots - lax.axis_index("gx") * per_pair
    )
    combos = 4 * send_slots
    pair_index = positions * send_slots + targets
    pair_match = pair_index[None, :] == jnp.arange(combos, dtype=jnp.int32)[:, None]
    pair_owner = jnp.sum(
        jnp.where(pair_match, jnp.arange(element_count, dtype=jnp.int32)[None, :], 0), 1
    ) + jnp.where(jnp.any(pair_match, 1), 0, element_count)
    face_src = jnp.moveaxis(
        face_sources.reshape(tile_rows, tile_cols, 3, functionals, face_dofs), 2, 0
    )
    coarse_source = lax.all_to_all(
        coarse_sources[:, 0, :].reshape(sources, per_pair, functionals, face_dofs),
        "gx",
        split_axis=0,
        concat_axis=0,
        tiled=True,
    ).reshape(send_slots, functionals, face_dofs)
    west_source = extended(face_src[0, -1:], (("gx", 0),), 1)[0]
    south_source = extended(face_src[1, :, -1:], (("gy", 1),), 1)[:, 0]

    def coarse_update(coarse_state, prev):
        top_flat = prev[5].reshape(element_count, functionals, face_dofs)
        padded_top = jnp.concatenate(
            [top_flat, jnp.zeros((1, functionals, face_dofs), jnp.float32)], 0
        )
        by_pair = jnp.take(padded_top, pair_owner, axis=0, mode="clip").reshape(
            4, send_slots, functionals, face_dofs
        )
        coarse_sum = jnp.einsum("ptfl,plk->tfk", by_pair, mortar_projection, precision=highest)
        return coarse_state + OMEGA * (coarse_source - coarse_sum)

    state = None
    coarse_state = OMEGA * coarse_source
    for sweep_index in range(1, ITERS):
        if state is not None:
            coarse_state = coarse_update(coarse_state, state[3])
        every_top = jnp.einsum(
            "tfk,plk->ptfl", coarse_state, mortar_projection, precision=highest
        ).reshape(combos, functionals, face_dofs)
        top_face = jnp.take(every_top, pair_index, axis=0, mode="clip").reshape(
            tile_rows, tile_cols, functionals, face_dofs
        )
        face_state, west_ghost, south_ghost, prev, to_w, to_e, to_s, to_n = sweep_call(
            count, state, face_src, west_source, south_source, top_face, element_blocks
        )
        state = (
            face_state,
            west_ghost,
            south_ghost,
            prev,
            to_previous(to_w, "gx"),
            to_next(to_e, "gx"),
            to_previous(to_s, "gy"),
            to_next(to_n, "gy"),
        )
    coarse_state = coarse_update(coarse_state, state[3])
    coarse_out = lax.all_to_all(
        coarse_state.reshape(sources, per_pair, trace_width),
        "gx",
        split_axis=0,
        concat_axis=0,
        tiled=True,
    )
    face_state, west_ghost, south_ghost, prev, from_e, from_w, from_n, from_s = state
    face_state = final_update(face_state, face_src, prev, from_e, from_n)
    face_out = jnp.moveaxis(face_state, 0, 2).reshape(tile_rows, tile_cols, 3, trace_width)
    coarse_out = coarse_out.reshape(owner_slots, 1, trace_width)
    return (face_out, coarse_out)


def solution(mesh):
    return jax.shard_map(
        shards,
        mesh=mesh,
        in_specs=(
            P("gx", "gy", None, None),
            P(),
            P("gx", "gy", None, None),
            P("gx", "gy", None),
            P("gx", "gy"),
            P("gx", "gy"),
            P("gx", "gy"),
        ),
        out_specs=(P("gx", "gy", None, None), P("gx", "gy", None)),
        check_vma=False,
    )
```

```python
import jax
import jax.numpy as jnp
from jax import lax
from jax.experimental import pallas as pl
from jax.experimental.pallas import tpu as pltpu
from jax.sharding import PartitionSpec as P

ITERS = 4


OMEGA = 0.8


def extended(cells, sides, width):
    for axis, dim in sides:
        count = lax.axis_size(axis)
        head = lax.slice_in_dim(cells, 0, width, axis=dim)
        tail = lax.slice_in_dim(cells, cells.shape[dim] - width, cells.shape[dim], axis=dim)
        cells = jnp.concatenate(
            [
                lax.ppermute(tail, axis, [(i, (i + 1) % count) for i in range(count)]),
                cells,
                lax.ppermute(head, axis, [((i + 1) % count, i) for i in range(count)]),
            ],
            axis=dim,
        )
    return cells


def to_next(block, axis):
    count = lax.axis_size(axis)
    return lax.ppermute(block, axis, [(i, (i + 1) % count) for i in range(count)])


def to_previous(block, axis):
    count = lax.axis_size(axis)
    return lax.ppermute(block, axis, [((i + 1) % count, i) for i in range(count)])


def apply_update(fs, src, wg, sg, wsrc, ssrc, prev, from_e, from_w, from_n, from_s, fs_o, wg_o, sg_o):
    rows, cols = fs.shape[1], fs.shape[2]
    for i in range(rows):
        neighbour = prev[0, i + 1] if i + 1 < rows else from_e[...]
        fs_o[0, i] = fs[0, i] + OMEGA * (src[0, i] - (prev[1, i] + neighbour))
    for j in range(cols):
        neighbour = prev[2, :, j + 1] if j + 1 < cols else from_n[...]
        fs_o[1, :, j] = fs[1, :, j] + OMEGA * (src[1, :, j] - (prev[3, :, j] + neighbour))
    fs_o[2] = fs[2] + OMEGA * (src[2] - prev[4])
    wg_o[...] = wg[...] + OMEGA * (wsrc[...] - (from_w[...] + prev[0, 0]))
    sg_o[...] = sg[...] + OMEGA * (ssrc[...] - (from_s[...] + prev[2, :, 0]))


def whole(shape):
    return pl.BlockSpec(shape, lambda *_: (0,) * len(shape))


def sweep_call(count, pair_index, state, src, wsrc, ssrc, every_top, blocks):
    _, rows, cols, functionals, face_dofs = src.shape
    width = blocks.shape[-1]

    def kernel(count_ref, pair_ref, *refs):
        if state is None:
            src_r, wsrc_r, ssrc_r, top_r, b_r = refs[:5]
        else:
            fs_r, wg_r, sg_r, prev_r, fe_r, fw_r, fn_r, fsr_r = refs[:8]
            src_r, wsrc_r, ssrc_r, top_r, b_r = refs[8:13]
        fs_o, wg_o, sg_o, c_o, ct_o, to_w, to_e, to_s, to_n = refs[-9:]
        i = pl.program_id(0)

        @pl.when(i == 0)
        def _():
            ct_o[...] = jnp.zeros(ct_o.shape, jnp.float32)
            if state is None:
                fs_o[...] = OMEGA * src_r[...]
                wg_o[...] = OMEGA * wsrc_r[...]
                sg_o[...] = OMEGA * ssrc_r[...]
            else:
                apply_update(fs_r, src_r, wg_r, sg_r, wsrc_r, ssrc_r, prev_r, fe_r, fw_r, fn_r,
                             fsr_r, fs_o, wg_o, sg_o)

        for j in range(cols):
            west = jnp.where(i == 0, wg_o[j], fs_o[0, jnp.maximum(i - 1, 0), j])
            south = sg_o[i] if j == 0 else fs_o[1, i, j - 1]
            pair = pair_ref[i * cols + j]
            row = jnp.concatenate(
                [west, fs_o[0, i, j], south, fs_o[1, i, j], fs_o[2, i, j], top_r[pair]], -1
            )
            out = jnp.dot(row.astype(jnp.bfloat16), b_r[0, j], preferred_element_type=jnp.float32)
            live = ((i * cols + j) < count_ref[0]).astype(jnp.float32)
            out = out * live
            for g in range(5):
                c_o[g, i, j] = out[:, g * face_dofs : (g + 1) * face_dofs]
            ct_o[pair] = out[:, 5 * face_dofs : 6 * face_dofs]
            if j == 0:
                to_s[i] = out[:, 2 * face_dofs : 3 * face_dofs]
            if j == cols - 1:
                to_n[i] = out[:, 3 * face_dofs : 4 * face_dofs]

        @pl.when(i == 0)
        def _():
            to_w[...] = c_o[0, 0]

        @pl.when(i == rows - 1)
        def _():
            to_e[...] = c_o[1, rows - 1]

    f32 = jnp.float32
    operands = (() if state is None else tuple(state)) + (src, wsrc, ssrc, every_top)
    out_shape = (
        jax.ShapeDtypeStruct(src.shape, f32),
        jax.ShapeDtypeStruct(wsrc.shape, f32),
        jax.ShapeDtypeStruct(ssrc.shape, f32),
        jax.ShapeDtypeStruct((5,) + src.shape[1:], f32),
        jax.ShapeDtypeStruct(every_top.shape, f32),
        jax.ShapeDtypeStruct(wsrc.shape, f32),
        jax.ShapeDtypeStruct(wsrc.shape, f32),
        jax.ShapeDtypeStruct(ssrc.shape, f32),
        jax.ShapeDtypeStruct(ssrc.shape, f32),
    )
    grid_spec = pltpu.PrefetchScalarGridSpec(
        num_scalar_prefetch=2,
        grid=(rows,),
        in_specs=[whole(a.shape) for a in operands]
        + [pl.BlockSpec((1, cols, width, width), lambda i, *_: (i, 0, 0, 0))],
        out_specs=[whole(s.shape) for s in out_shape],
    )
    return pl.pallas_call(kernel, grid_spec=grid_spec, out_shape=out_shape)(
        count, pair_index, *operands, blocks
    )


def final_update(fs, src, wg, sg, wsrc, ssrc, prev, from_e, from_w, from_n, from_s):
    def kernel(fs_r, src_r, wg_r, sg_r, wsrc_r, ssrc_r, prev_r, fe_r, fw_r, fn_r, fsr_r,
               fs_o, wg_o, sg_o):
        apply_update(fs_r, src_r, wg_r, sg_r, wsrc_r, ssrc_r, prev_r, fe_r, fw_r, fn_r, fsr_r,
                     fs_o, wg_o, sg_o)

    f32 = jnp.float32
    out_shape = (
        jax.ShapeDtypeStruct(fs.shape, f32),
        jax.ShapeDtypeStruct(wg.shape, f32),
        jax.ShapeDtypeStruct(sg.shape, f32),
    )
    return pl.pallas_call(kernel, out_shape=out_shape)(
        fs, src, wg, sg, wsrc, ssrc, prev, from_e, from_w, from_n, from_s
    )[0]


def shards(
    element_blocks,
    mortar_projection,
    face_sources,
    coarse_sources,
    parent_slot,
    child_position,
    live_count,
):
    highest = lax.Precision.HIGHEST
    tile_rows, tile_cols = parent_slot.shape
    trace_width = face_sources.shape[-1]
    face_dofs = mortar_projection.shape[-1]
    functionals = trace_width // face_dofs
    sources = lax.axis_size("gx")
    owner_slots = coarse_sources.shape[0]
    per_pair = owner_slots // sources
    element_count = tile_rows * tile_cols
    send_slots = sources * per_pair
    count = live_count.reshape(1)
    parents = parent_slot.reshape(element_count)
    positions = child_position.reshape(element_count)
    targets = (
        parents // owner_slots * per_pair + parents % owner_slots - lax.axis_index("gx") * per_pair
    )
    combos = 4 * send_slots
    pair_index = positions * send_slots + targets
    face_src = jnp.moveaxis(
        face_sources.reshape(tile_rows, tile_cols, 3, functionals, face_dofs), 2, 0
    )
    coarse_source = lax.all_to_all(
        coarse_sources[:, 0, :].reshape(sources, per_pair, functionals, face_dofs),
        "gx",
        split_axis=0,
        concat_axis=0,
        tiled=True,
    ).reshape(send_slots, functionals, face_dofs)
    west_source = extended(face_src[0, -1:], (("gx", 0),), 1)[0]
    south_source = extended(face_src[1, :, -1:], (("gy", 1),), 1)[:, 0]

    def coarse_update(coarse_state, by_pair):
        by_pair = by_pair.reshape(4, send_slots, functionals, face_dofs)
        coarse_sum = jnp.einsum("ptfl,plk->tfk", by_pair, mortar_projection, precision=highest)
        return coarse_state + OMEGA * (coarse_source - coarse_sum)

    state = None
    coarse_state = OMEGA * coarse_source
    for sweep_index in range(1, ITERS):
        if state is not None:
            coarse_state = coarse_update(coarse_state, by_pair)
        every_top = jnp.einsum(
            "tfk,plk->ptfl", coarse_state, mortar_projection, precision=highest
        ).reshape(combos, functionals, face_dofs)
        face_state, west_ghost, south_ghost, prev, by_pair, to_w, to_e, to_s, to_n = sweep_call(
            count, pair_index, state, face_src, west_source, south_source, every_top,
            element_blocks,
        )
        state = (
            face_state,
            west_ghost,
            south_ghost,
            prev,
            to_previous(to_w, "gx"),
            to_next(to_e, "gx"),
            to_previous(to_s, "gy"),
            to_next(to_n, "gy"),
        )
    coarse_state = coarse_update(coarse_state, by_pair)
    coarse_out = lax.all_to_all(
        coarse_state.reshape(sources, per_pair, functionals, face_dofs),
        "gx",
        split_axis=0,
        concat_axis=0,
        tiled=True,
    )
    face_state, west_ghost, south_ghost, prev, from_e, from_w, from_n, from_s = state
    face_state = final_update(
        face_state, face_src, west_ghost, south_ghost, west_source, south_source,
        prev, from_e, from_w, from_n, from_s,
    )
    face_out = jnp.moveaxis(face_state, 0, 2).reshape(tile_rows, tile_cols, 3, trace_width)
    coarse_out = coarse_out.reshape(owner_slots, 1, trace_width)
    return (face_out, coarse_out)


def solution(mesh):
    return jax.shard_map(
        shards,
        mesh=mesh,
        in_specs=(
            P("gx", "gy", None, None),
            P(),
            P("gx", "gy", None, None),
            P("gx", "gy", None),
            P("gx", "gy"),
            P("gx", "gy"),
            P("gx", "gy"),
        ),
        out_specs=(P("gx", "gy", None, None), P("gx", "gy", None)),
        check_vma=False,
    )
```

```python
import jax
import jax.numpy as jnp
from jax import lax
from jax.experimental import pallas as pl
from jax.experimental.pallas import tpu as pltpu
from jax.sharding import PartitionSpec as P

ITERS = 4


OMEGA = 0.8


def extended(cells, sides, width):
    for axis, dim in sides:
        count = lax.axis_size(axis)
        head = lax.slice_in_dim(cells, 0, width, axis=dim)
        tail = lax.slice_in_dim(cells, cells.shape[dim] - width, cells.shape[dim], axis=dim)
        cells = jnp.concatenate(
            [
                lax.ppermute(tail, axis, [(i, (i + 1) % count) for i in range(count)]),
                cells,
                lax.ppermute(head, axis, [((i + 1) % count, i) for i in range(count)]),
            ],
            axis=dim,
        )
    return cells


def to_next(block, axis):
    count = lax.axis_size(axis)
    return lax.ppermute(block, axis, [(i, (i + 1) % count) for i in range(count)])


def to_previous(block, axis):
    count = lax.axis_size(axis)
    return lax.ppermute(block, axis, [((i + 1) % count, i) for i in range(count)])


def whole(shape):
    return pl.BlockSpec(shape, lambda *_: (0,) * len(shape))


def sweep_call(count, state, src, wsrc, ssrc, top, blocks):
    _, rows, cols, functionals, face_dofs = src.shape
    width = blocks.shape[-1]

    def kernel(count_ref, *refs):
        if state is None:
            src_r, wsrc_r, ssrc_r, top_r, b_r = refs[:5]
        else:
            fs_r, wg_r, sg_r, tw_r, te_r, ts_r, tn_r, fe_r, fw_r, fn_r, fsr_r = refs[:11]
            src_r, wsrc_r, ssrc_r, top_r, b_r = refs[11:16]
        fs_o, wg_o, sg_o, ct_o, to_w, to_e, to_s, to_n, c_v = refs[-9:]
        i = pl.program_id(0)

        @pl.when(i == 0)
        def _():
            if state is None:
                fs_o[...] = OMEGA * src_r[...]
                wg_o[...] = OMEGA * wsrc_r[...]
                sg_o[...] = OMEGA * ssrc_r[...]
            else:
                fs_o[...] = fs_r[...]
                fs_o[0, rows - 1] = fs_r[0, rows - 1] + OMEGA * (
                    src_r[0, rows - 1] - (te_r[...] + fe_r[...])
                )
                fs_o[1, :, cols - 1] = fs_r[1, :, cols - 1] + OMEGA * (
                    src_r[1, :, cols - 1] - (tn_r[...] + fn_r[...])
                )
                wg_o[...] = wg_r[...] + OMEGA * (wsrc_r[...] - (fw_r[...] + tw_r[...]))
                sg_o[...] = sg_r[...] + OMEGA * (ssrc_r[...] - (fsr_r[...] + ts_r[...]))

        for j in range(cols):
            west = jnp.where(i == 0, wg_o[j], fs_o[0, jnp.maximum(i - 1, 0), j])
            south = sg_o[i] if j == 0 else fs_o[1, i, j - 1]
            row = jnp.concatenate(
                [west, fs_o[0, i, j], south, fs_o[1, i, j], fs_o[2, i, j], top_r[i, j]], -1
            )
            out = jnp.dot(row.astype(jnp.bfloat16), b_r[0, j], preferred_element_type=jnp.float32)
            live = ((i * cols + j) < count_ref[0]).astype(jnp.float32)
            out = out * live
            for g in range(5):
                c_v[g, i, j] = out[:, g * face_dofs : (g + 1) * face_dofs]
            ct_o[i, j] = out[:, 5 * face_dofs : 6 * face_dofs]
            if j == 0:
                to_s[i] = out[:, 2 * face_dofs : 3 * face_dofs]
            if j == cols - 1:
                to_n[i] = out[:, 3 * face_dofs : 4 * face_dofs]

            @pl.when(i == 0)
            def _():
                to_w[j] = out[:, 0:face_dofs]

            @pl.when(i == rows - 1)
            def _():
                to_e[j] = out[:, face_dofs : 2 * face_dofs]

        @pl.when(i == rows - 1)
        def _():
            for r in range(rows - 1):
                fs_o[0, r] = fs_o[0, r] + OMEGA * (src_r[0, r] - (c_v[1, r] + c_v[0, r + 1]))
            for c in range(cols - 1):
                fs_o[1, :, c] = fs_o[1, :, c] + OMEGA * (
                    src_r[1, :, c] - (c_v[3, :, c] + c_v[2, :, c + 1])
                )
            fs_o[2] = fs_o[2] + OMEGA * (src_r[2] - c_v[4])

    f32 = jnp.float32
    operands = (() if state is None else tuple(state)) + (src, wsrc, ssrc, top)
    out_shape = (
        jax.ShapeDtypeStruct(src.shape, f32),
        jax.ShapeDtypeStruct(wsrc.shape, f32),
        jax.ShapeDtypeStruct(ssrc.shape, f32),
        jax.ShapeDtypeStruct(top.shape, f32),
        jax.ShapeDtypeStruct(wsrc.shape, f32),
        jax.ShapeDtypeStruct(wsrc.shape, f32),
        jax.ShapeDtypeStruct(ssrc.shape, f32),
        jax.ShapeDtypeStruct(ssrc.shape, f32),
    )
    grid_spec = pltpu.PrefetchScalarGridSpec(
        num_scalar_prefetch=1,
        grid=(rows,),
        in_specs=[whole(a.shape) for a in operands]
        + [pl.BlockSpec((1, cols, width, width), lambda i, *_: (i, 0, 0, 0))],
        out_specs=[whole(s.shape) for s in out_shape],
        scratch_shapes=[pltpu.VMEM((5,) + src.shape[1:], f32)],
    )
    return pl.pallas_call(kernel, grid_spec=grid_spec, out_shape=out_shape)(
        count, *operands, blocks
    )


def shards(
    element_blocks,
    mortar_projection,
    face_sources,
    coarse_sources,
    parent_slot,
    child_position,
    live_count,
):
    highest = lax.Precision.HIGHEST
    tile_rows, tile_cols = parent_slot.shape
    trace_width = face_sources.shape[-1]
    face_dofs = mortar_projection.shape[-1]
    functionals = trace_width // face_dofs
    sources = lax.axis_size("gx")
    owner_slots = coarse_sources.shape[0]
    per_pair = owner_slots // sources
    element_count = tile_rows * tile_cols
    send_slots = sources * per_pair
    count = live_count.reshape(1)
    parents = parent_slot.reshape(element_count)
    positions = child_position.reshape(element_count)
    targets = (
        parents // owner_slots * per_pair + parents % owner_slots - lax.axis_index("gx") * per_pair
    )
    combos = 4 * send_slots
    pair_index = positions * send_slots + targets
    pair_match = pair_index[None, :] == jnp.arange(combos, dtype=jnp.int32)[:, None]
    pair_owner = jnp.sum(
        jnp.where(pair_match, jnp.arange(element_count, dtype=jnp.int32)[None, :], 0), 1
    ) + jnp.where(jnp.any(pair_match, 1), 0, element_count)
    face_src = jnp.moveaxis(
        face_sources.reshape(tile_rows, tile_cols, 3, functionals, face_dofs), 2, 0
    )
    coarse_source = lax.all_to_all(
        coarse_sources[:, 0, :].reshape(sources, per_pair, functionals, face_dofs),
        "gx",
        split_axis=0,
        concat_axis=0,
        tiled=True,
    ).reshape(send_slots, functionals, face_dofs)
    west_source = extended(face_src[0, -1:], (("gx", 0),), 1)[0]
    south_source = extended(face_src[1, :, -1:], (("gy", 1),), 1)[:, 0]

    def coarse_update(coarse_state, prev):
        top_flat = prev.reshape(element_count, functionals, face_dofs)
        padded_top = jnp.concatenate(
            [top_flat, jnp.zeros((1, functionals, face_dofs), jnp.float32)], 0
        )
        by_pair = jnp.take(padded_top, pair_owner, axis=0, mode="clip").reshape(
            4, send_slots, functionals, face_dofs
        )
        coarse_sum = jnp.einsum("ptfl,plk->tfk", by_pair, mortar_projection, precision=highest)
        return coarse_state + OMEGA * (coarse_source - coarse_sum)

    state = None
    coarse_state = OMEGA * coarse_source
    for sweep_index in range(1, ITERS):
        if state is not None:
            coarse_state = coarse_update(coarse_state, coarse_part)
        every_top = jnp.einsum(
            "tfk,plk->ptfl", coarse_state, mortar_projection, precision=highest
        ).reshape(combos, functionals, face_dofs)
        top_face = jnp.take(every_top, pair_index, axis=0, mode="clip").reshape(
            tile_rows, tile_cols, functionals, face_dofs
        )
        face_state, west_ghost, south_ghost, coarse_part, to_w, to_e, to_s, to_n = sweep_call(
            count, state, face_src, west_source, south_source, top_face, element_blocks
        )
        from_e = to_previous(to_w, "gx")
        from_n = to_previous(to_s, "gy")
        state = (
            face_state,
            west_ghost,
            south_ghost,
            to_w,
            to_e,
            to_s,
            to_n,
            from_e,
            to_next(to_e, "gx"),
            from_n,
            to_next(to_n, "gy"),
        )
    coarse_state = coarse_update(coarse_state, coarse_part)
    coarse_out = lax.all_to_all(
        coarse_state.reshape(sources, per_pair, functionals, face_dofs),
        "gx",
        split_axis=0,
        concat_axis=0,
        tiled=True,
    )
    east_last = face_state[0, -1] + OMEGA * (face_src[0, -1] - (to_e + from_e))
    north_last = face_state[1, :, -1] + OMEGA * (face_src[1, :, -1] - (to_n + from_n))
    face_state = face_state.at[0, -1].set(east_last).at[1, :, -1].set(north_last)
    face_out = jnp.moveaxis(face_state, 0, 2).reshape(tile_rows, tile_cols, 3, trace_width)
    coarse_out = coarse_out.reshape(owner_slots, 1, trace_width)
    return (face_out, coarse_out)


def solution(mesh):
    return jax.shard_map(
        shards,
        mesh=mesh,
        in_specs=(
            P("gx", "gy", None, None),
            P(),
            P("gx", "gy", None, None),
            P("gx", "gy", None),
            P("gx", "gy"),
            P("gx", "gy"),
            P("gx", "gy"),
        ),
        out_specs=(P("gx", "gy", None, None), P("gx", "gy", None)),
        check_vma=False,
    )
```

```python
import jax
import jax.numpy as jnp
from jax import lax
from jax.experimental import pallas as pl
from jax.experimental.pallas import tpu as pltpu
from jax.sharding import PartitionSpec as P

ITERS = 4


OMEGA = 0.8


def extended(cells, sides, width):
    for axis, dim in sides:
        count = lax.axis_size(axis)
        head = lax.slice_in_dim(cells, 0, width, axis=dim)
        tail = lax.slice_in_dim(cells, cells.shape[dim] - width, cells.shape[dim], axis=dim)
        cells = jnp.concatenate(
            [
                lax.ppermute(tail, axis, [(i, (i + 1) % count) for i in range(count)]),
                cells,
                lax.ppermute(head, axis, [((i + 1) % count, i) for i in range(count)]),
            ],
            axis=dim,
        )
    return cells


def to_next(block, axis):
    count = lax.axis_size(axis)
    return lax.ppermute(block, axis, [(i, (i + 1) % count) for i in range(count)])


def to_previous(block, axis):
    count = lax.axis_size(axis)
    return lax.ppermute(block, axis, [((i + 1) % count, i) for i in range(count)])


def apply_update(fs, src, wg, sg, wsrc, ssrc, prev, from_e, from_w, from_n, from_s, fs_o, wg_o, sg_o):
    rows, cols = fs.shape[1], fs.shape[2]
    for i in range(rows):
        neighbour = prev[0, i + 1] if i + 1 < rows else from_e[...]
        fs_o[0, i] = fs[0, i] + OMEGA * (src[0, i] - (prev[1, i] + neighbour))
    for j in range(cols):
        neighbour = prev[2, :, j + 1] if j + 1 < cols else from_n[...]
        fs_o[1, :, j] = fs[1, :, j] + OMEGA * (src[1, :, j] - (prev[3, :, j] + neighbour))
    fs_o[2] = fs[2] + OMEGA * (src[2] - prev[4])
    wg_o[...] = wg[...] + OMEGA * (wsrc[...] - (from_w[...] + prev[0, 0]))
    sg_o[...] = sg[...] + OMEGA * (ssrc[...] - (from_s[...] + prev[2, :, 0]))


def whole(shape):
    return pl.BlockSpec(shape, lambda *_: (0,) * len(shape))


def sweep_call(count, state, src, wsrc, ssrc, top, blocks):
    _, rows, cols, functionals, face_dofs = src.shape
    width = blocks.shape[-1]
    per_step = 2 if rows % 2 == 0 else 1

    def kernel(count_ref, *refs):
        if state is None:
            src_r, wsrc_r, ssrc_r, top_r, b_r = refs[:5]
        else:
            fs_r, wg_r, sg_r, prev_r, fe_r, fw_r, fn_r, fsr_r = refs[:8]
            src_r, wsrc_r, ssrc_r, top_r, b_r = refs[8:13]
        fs_o, wg_o, sg_o, c_o, to_w, to_e, to_s, to_n = refs[-8:]
        step = pl.program_id(0)

        @pl.when(step == 0)
        def _():
            if state is None:
                fs_o[...] = OMEGA * src_r[...]
                wg_o[...] = OMEGA * wsrc_r[...]
                sg_o[...] = OMEGA * ssrc_r[...]
            else:
                apply_update(fs_r, src_r, wg_r, sg_r, wsrc_r, ssrc_r, prev_r, fe_r, fw_r, fn_r,
                             fsr_r, fs_o, wg_o, sg_o)

        for r, j in [(r, j) for r in range(per_step) for j in range(cols)]:
            i = step * per_step + r
            west = jnp.where(i == 0, wg_o[j], fs_o[0, jnp.maximum(i - 1, 0), j])
            south = sg_o[i] if j == 0 else fs_o[1, i, j - 1]
            row = jnp.concatenate(
                [west, fs_o[0, i, j], south, fs_o[1, i, j], fs_o[2, i, j], top_r[i, j]], -1
            )
            out = jnp.dot(row.astype(jnp.bfloat16), b_r[r, j], preferred_element_type=jnp.float32)
            live = ((i * cols + j) < count_ref[0]).astype(jnp.float32)
            out = out * live
            for g in range(6):
                c_o[g, i, j] = out[:, g * face_dofs : (g + 1) * face_dofs]
            if j == 0:
                to_s[i] = out[:, 2 * face_dofs : 3 * face_dofs]
            if j == cols - 1:
                to_n[i] = out[:, 3 * face_dofs : 4 * face_dofs]

        @pl.when(step == 0)
        def _():
            to_w[...] = c_o[0, 0]

        @pl.when(step == rows // per_step - 1)
        def _():
            to_e[...] = c_o[1, rows - 1]

    f32 = jnp.float32
    operands = (() if state is None else tuple(state)) + (src, wsrc, ssrc, top)
    prev = None if state is None else state[3]
    out_shape = (
        jax.ShapeDtypeStruct(src.shape, f32),
        jax.ShapeDtypeStruct(wsrc.shape, f32),
        jax.ShapeDtypeStruct(ssrc.shape, f32),
        jax.ShapeDtypeStruct((6,) + src.shape[1:], f32),
        jax.ShapeDtypeStruct(wsrc.shape, f32),
        jax.ShapeDtypeStruct(wsrc.shape, f32),
        jax.ShapeDtypeStruct(ssrc.shape, f32),
        jax.ShapeDtypeStruct(ssrc.shape, f32),
    )
    specs = [whole(a.shape) for a in operands]
    if state is not None:
        specs[3] = whole((5,) + prev.shape[1:])
    grid_spec = pltpu.PrefetchScalarGridSpec(
        num_scalar_prefetch=1,
        grid=(rows // per_step,),
        in_specs=specs
        + [pl.BlockSpec((per_step, cols, width, width), lambda i, *_: (i, 0, 0, 0))],
        out_specs=[whole(s.shape) for s in out_shape],
    )
    return pl.pallas_call(kernel, grid_spec=grid_spec, out_shape=out_shape)(
        count, *operands, blocks
    )


def final_update(fs, src, wg, sg, wsrc, ssrc, prev, from_e, from_w, from_n, from_s):
    def kernel(fs_r, src_r, wg_r, sg_r, wsrc_r, ssrc_r, prev_r, fe_r, fw_r, fn_r, fsr_r,
               fs_o, wg_o, sg_o):
        apply_update(fs_r, src_r, wg_r, sg_r, wsrc_r, ssrc_r, prev_r, fe_r, fw_r, fn_r, fsr_r,
                     fs_o, wg_o, sg_o)

    f32 = jnp.float32
    out_shape = (
        jax.ShapeDtypeStruct(fs.shape, f32),
        jax.ShapeDtypeStruct(wg.shape, f32),
        jax.ShapeDtypeStruct(sg.shape, f32),
    )
    return pl.pallas_call(kernel, out_shape=out_shape)(
        fs, src, wg, sg, wsrc, ssrc, prev, from_e, from_w, from_n, from_s
    )[0]


def shards(
    element_blocks,
    mortar_projection,
    face_sources,
    coarse_sources,
    parent_slot,
    child_position,
    live_count,
):
    highest = lax.Precision.HIGHEST
    tile_rows, tile_cols = parent_slot.shape
    trace_width = face_sources.shape[-1]
    face_dofs = mortar_projection.shape[-1]
    functionals = trace_width // face_dofs
    sources = lax.axis_size("gx")
    owner_slots = coarse_sources.shape[0]
    per_pair = owner_slots // sources
    element_count = tile_rows * tile_cols
    send_slots = sources * per_pair
    count = live_count.reshape(1)
    parents = parent_slot.reshape(element_count)
    positions = child_position.reshape(element_count)
    targets = (
        parents // owner_slots * per_pair + parents % owner_slots - lax.axis_index("gx") * per_pair
    )
    combos = 4 * send_slots
    pair_index = positions * send_slots + targets
    pair_match = pair_index[None, :] == jnp.arange(combos, dtype=jnp.int32)[:, None]
    pair_owner = jnp.sum(
        jnp.where(pair_match, jnp.arange(element_count, dtype=jnp.int32)[None, :], 0), 1
    ) + jnp.where(jnp.any(pair_match, 1), 0, element_count)
    face_src = jnp.moveaxis(
        face_sources.reshape(tile_rows, tile_cols, 3, functionals, face_dofs), 2, 0
    )
    coarse_source = lax.all_to_all(
        coarse_sources[:, 0, :].reshape(sources, per_pair, functionals, face_dofs),
        "gx",
        split_axis=0,
        concat_axis=0,
        tiled=True,
    ).reshape(send_slots, functionals, face_dofs)
    west_source = extended(face_src[0, -1:], (("gx", 0),), 1)[0]
    south_source = extended(face_src[1, :, -1:], (("gy", 1),), 1)[:, 0]

    def coarse_update(coarse_state, prev):
        top_flat = prev[5].reshape(element_count, functionals, face_dofs)
        padded_top = jnp.concatenate(
            [top_flat, jnp.zeros((1, functionals, face_dofs), jnp.float32)], 0
        )
        by_pair = jnp.take(padded_top, pair_owner, axis=0, mode="clip").reshape(
            4, send_slots, functionals, face_dofs
        )
        coarse_sum = jnp.einsum("ptfl,plk->tfk", by_pair, mortar_projection, precision=highest)
        return coarse_state + OMEGA * (coarse_source - coarse_sum)

    state = None
    coarse_state = OMEGA * coarse_source
    for sweep_index in range(1, ITERS):
        if state is not None:
            coarse_state = coarse_update(coarse_state, state[3])
        every_top = jnp.einsum(
            "tfk,plk->ptfl", coarse_state, mortar_projection, precision=highest
        ).reshape(combos, functionals, face_dofs)
        top_face = jnp.take(every_top, pair_index, axis=0, mode="clip").reshape(
            tile_rows, tile_cols, functionals, face_dofs
        )
        face_state, west_ghost, south_ghost, prev, to_w, to_e, to_s, to_n = sweep_call(
            count, state, face_src, west_source, south_source, top_face, element_blocks
        )
        state = (
            face_state,
            west_ghost,
            south_ghost,
            prev,
            to_previous(to_w, "gx"),
            to_next(to_e, "gx"),
            to_previous(to_s, "gy"),
            to_next(to_n, "gy"),
        )
    coarse_state = coarse_update(coarse_state, state[3])
    coarse_out = lax.all_to_all(
        coarse_state.reshape(sources, per_pair, functionals, face_dofs),
        "gx",
        split_axis=0,
        concat_axis=0,
        tiled=True,
    )
    face_state, west_ghost, south_ghost, prev, from_e, from_w, from_n, from_s = state
    face_state = final_update(
        face_state, face_src, west_ghost, south_ghost, west_source, south_source,
        prev, from_e, from_w, from_n, from_s,
    )
    face_out = jnp.moveaxis(face_state, 0, 2).reshape(tile_rows, tile_cols, 3, trace_width)
    coarse_out = coarse_out.reshape(owner_slots, 1, trace_width)
    return (face_out, coarse_out)


def solution(mesh):
    return jax.shard_map(
        shards,
        mesh=mesh,
        in_specs=(
            P("gx", "gy", None, None),
            P(),
            P("gx", "gy", None, None),
            P("gx", "gy", None),
            P("gx", "gy"),
            P("gx", "gy"),
            P("gx", "gy"),
        ),
        out_specs=(P("gx", "gy", None, None), P("gx", "gy", None)),
        check_vma=False,
    )
```

```python
import jax
import jax.numpy as jnp
from jax import lax
from jax.experimental import pallas as pl
from jax.experimental.pallas import tpu as pltpu
from jax.sharding import PartitionSpec as P

ITERS = 4


OMEGA = 0.8


def extended(cells, sides, width):
    for axis, dim in sides:
        count = lax.axis_size(axis)
        head = lax.slice_in_dim(cells, 0, width, axis=dim)
        tail = lax.slice_in_dim(cells, cells.shape[dim] - width, cells.shape[dim], axis=dim)
        cells = jnp.concatenate(
            [
                lax.ppermute(tail, axis, [(i, (i + 1) % count) for i in range(count)]),
                cells,
                lax.ppermute(head, axis, [((i + 1) % count, i) for i in range(count)]),
            ],
            axis=dim,
        )
    return cells


def to_next(block, axis):
    count = lax.axis_size(axis)
    return lax.ppermute(block, axis, [(i, (i + 1) % count) for i in range(count)])


def to_previous(block, axis):
    count = lax.axis_size(axis)
    return lax.ppermute(block, axis, [((i + 1) % count, i) for i in range(count)])


def apply_update(fs, src, wg, sg, wsrc, ssrc, prev, from_e, from_w, from_n, from_s, fs_o, wg_o, sg_o):
    rows, cols = fs.shape[1], fs.shape[2]
    for i in range(rows):
        neighbour = prev[0, i + 1] if i + 1 < rows else from_e[...]
        fs_o[0, i] = fs[0, i] + OMEGA * (src[0, i] - (prev[1, i] + neighbour))
    for j in range(cols):
        neighbour = prev[2, :, j + 1] if j + 1 < cols else from_n[...]
        fs_o[1, :, j] = fs[1, :, j] + OMEGA * (src[1, :, j] - (prev[3, :, j] + neighbour))
    fs_o[2] = fs[2] + OMEGA * (src[2] - prev[4])
    wg_o[...] = wg[...] + OMEGA * (wsrc[...] - (from_w[...] + prev[0, 0]))
    sg_o[...] = sg[...] + OMEGA * (ssrc[...] - (from_s[...] + prev[2, :, 0]))


def whole(shape):
    return pl.BlockSpec(shape, lambda *_: (0,) * len(shape))


def sweep_call(count, state, src, wsrc, ssrc, top, blocks):
    _, rows, cols, functionals, face_dofs = src.shape
    width = blocks.shape[-1]
    per_step = 2 if rows % 2 == 0 else 1

    def kernel(count_ref, *refs):
        if state is None:
            src_r, wsrc_r, ssrc_r, top_r, b_r = refs[:5]
        else:
            fs_r, wg_r, sg_r, prev_r, fe_r, fw_r, fn_r, fsr_r = refs[:8]
            src_r, wsrc_r, ssrc_r, top_r, b_r = refs[8:13]
        fs_o, wg_o, sg_o, c_o, to_w, to_e, to_s, to_n = refs[-8:]
        step = pl.program_id(0)

        @pl.when(step == 0)
        def _():
            if state is None:
                fs_o[...] = OMEGA * src_r[...]
                wg_o[...] = OMEGA * wsrc_r[...]
                sg_o[...] = OMEGA * ssrc_r[...]
            else:
                apply_update(fs_r, src_r, wg_r, sg_r, wsrc_r, ssrc_r, prev_r, fe_r, fw_r, fn_r,
                             fsr_r, fs_o, wg_o, sg_o)

        for r, j in [(r, j) for r in range(per_step) for j in range(cols)]:
            i = step * per_step + r
            west = jnp.where(i == 0, wg_o[j], fs_o[0, jnp.maximum(i - 1, 0), j])
            south = sg_o[i] if j == 0 else fs_o[1, i, j - 1]
            row = jnp.concatenate(
                [west, fs_o[0, i, j], south, fs_o[1, i, j], fs_o[2, i, j], top_r[i, j]], -1
            )
            out = jnp.dot(row.astype(jnp.bfloat16), b_r[r, j], preferred_element_type=jnp.float32)
            live = ((i * cols + j) < count_ref[0]).astype(jnp.float32)
            out = out * live
            for g in range(6):
                c_o[g, i, j] = out[:, g * face_dofs : (g + 1) * face_dofs]
            if j == 0:
                to_s[i] = out[:, 2 * face_dofs : 3 * face_dofs]
            if j == cols - 1:
                to_n[i] = out[:, 3 * face_dofs : 4 * face_dofs]

        @pl.when(step == 0)
        def _():
            to_w[...] = c_o[0, 0]

        @pl.when(step == rows // per_step - 1)
        def _():
            to_e[...] = c_o[1, rows - 1]

    f32 = jnp.float32
    operands = (() if state is None else tuple(state)) + (src, wsrc, ssrc, top)
    prev = None if state is None else state[3]
    out_shape = (
        jax.ShapeDtypeStruct(src.shape, f32),
        jax.ShapeDtypeStruct(wsrc.shape, f32),
        jax.ShapeDtypeStruct(ssrc.shape, f32),
        jax.ShapeDtypeStruct((6,) + src.shape[1:], f32),
        jax.ShapeDtypeStruct(wsrc.shape, f32),
        jax.ShapeDtypeStruct(wsrc.shape, f32),
        jax.ShapeDtypeStruct(ssrc.shape, f32),
        jax.ShapeDtypeStruct(ssrc.shape, f32),
    )
    specs = [whole(a.shape) for a in operands]
    if state is not None:
        specs[3] = whole((5,) + prev.shape[1:])
    grid_spec = pltpu.PrefetchScalarGridSpec(
        num_scalar_prefetch=1,
        grid=(rows // per_step,),
        in_specs=specs
        + [pl.BlockSpec((per_step, cols, width, width), lambda i, *_: (i, 0, 0, 0))],
        out_specs=[whole(s.shape) for s in out_shape],
    )
    return pl.pallas_call(kernel, grid_spec=grid_spec, out_shape=out_shape)(
        count, *operands, blocks
    )


def final_update(fs, src, prev):
    _, rows, cols, functionals, face_dofs = fs.shape

    def kernel(fs_r, src_r, prev_r, fs_o):
        for i in range(rows):
            if i + 1 < rows:
                fs_o[i, 0] = fs_r[0, i] + OMEGA * (src_r[0, i] - (prev_r[1, i] + prev_r[0, i + 1]))
            else:
                fs_o[i, 0] = fs_r[0, i]
            for j in range(cols):
                if j + 1 < cols:
                    fs_o[i, 1, j] = fs_r[1, i, j] + OMEGA * (
                        src_r[1, i, j] - (prev_r[3, i, j] + prev_r[2, i, j + 1])
                    )
                else:
                    fs_o[i, 1, j] = fs_r[1, i, j]
            fs_o[i, 2] = fs_r[2, i] + OMEGA * (src_r[2, i] - prev_r[4, i])

    return pl.pallas_call(
        kernel,
        grid=(1,),
        in_specs=[whole(fs.shape), whole(src.shape), whole((5,) + prev.shape[1:])],
        out_specs=whole((rows, 3, cols, functionals, face_dofs)),
        out_shape=jax.ShapeDtypeStruct((rows, 3, cols, functionals, face_dofs), jnp.float32),
    )(fs, src, prev)


def shards(
    element_blocks,
    mortar_projection,
    face_sources,
    coarse_sources,
    parent_slot,
    child_position,
    live_count,
):
    highest = lax.Precision.HIGHEST
    tile_rows, tile_cols = parent_slot.shape
    trace_width = face_sources.shape[-1]
    face_dofs = mortar_projection.shape[-1]
    functionals = trace_width // face_dofs
    sources = lax.axis_size("gx")
    owner_slots = coarse_sources.shape[0]
    per_pair = owner_slots // sources
    element_count = tile_rows * tile_cols
    send_slots = sources * per_pair
    count = live_count.reshape(1)
    parents = parent_slot.reshape(element_count)
    positions = child_position.reshape(element_count)
    targets = (
        parents // owner_slots * per_pair + parents % owner_slots - lax.axis_index("gx") * per_pair
    )
    combos = 4 * send_slots
    pair_index = positions * send_slots + targets
    pair_match = pair_index[None, :] == jnp.arange(combos, dtype=jnp.int32)[:, None]
    pair_owner = jnp.sum(
        jnp.where(pair_match, jnp.arange(element_count, dtype=jnp.int32)[None, :], 0), 1
    ) + jnp.where(jnp.any(pair_match, 1), 0, element_count)
    face_src = jnp.moveaxis(
        face_sources.reshape(tile_rows, tile_cols, 3, functionals, face_dofs), 2, 0
    )
    coarse_source = lax.all_to_all(
        coarse_sources[:, 0, :].reshape(sources, per_pair, functionals, face_dofs),
        "gx",
        split_axis=0,
        concat_axis=0,
        tiled=True,
    ).reshape(send_slots, functionals, face_dofs)
    west_source = extended(face_src[0, -1:], (("gx", 0),), 1)[0]
    south_source = extended(face_src[1, :, -1:], (("gy", 1),), 1)[:, 0]

    def coarse_update(coarse_state, prev):
        top_flat = prev[5].reshape(element_count, functionals, face_dofs)
        padded_top = jnp.concatenate(
            [top_flat, jnp.zeros((1, functionals, face_dofs), jnp.float32)], 0
        )
        by_pair = jnp.take(padded_top, pair_owner, axis=0, mode="clip").reshape(
            4, send_slots, functionals, face_dofs
        )
        coarse_sum = jnp.einsum("ptfl,plk->tfk", by_pair, mortar_projection, precision=highest)
        return coarse_state + OMEGA * (coarse_source - coarse_sum)

    state = None
    coarse_state = OMEGA * coarse_source
    for sweep_index in range(1, ITERS):
        if state is not None:
            coarse_state = coarse_update(coarse_state, state[3])
        every_top = jnp.einsum(
            "tfk,plk->ptfl", coarse_state, mortar_projection, precision=highest
        ).reshape(combos, functionals, face_dofs)
        top_face = jnp.take(every_top, pair_index, axis=0, mode="clip").reshape(
            tile_rows, tile_cols, functionals, face_dofs
        )
        face_state, west_ghost, south_ghost, prev, to_w, to_e, to_s, to_n = sweep_call(
            count, state, face_src, west_source, south_source, top_face, element_blocks
        )
        state = (
            face_state,
            west_ghost,
            south_ghost,
            prev,
            to_previous(to_w, "gx"),
            to_next(to_e, "gx"),
            to_previous(to_s, "gy"),
            to_next(to_n, "gy"),
        )
    coarse_state = coarse_update(coarse_state, state[3])
    coarse_out = lax.all_to_all(
        coarse_state.reshape(sources, per_pair, functionals, face_dofs),
        "gx",
        split_axis=0,
        concat_axis=0,
        tiled=True,
    )
    face_state, west_ghost, south_ghost, prev, from_e, from_w, from_n, from_s = state
    inner = final_update(face_state, face_src, prev)
    east_last = face_state[0, -1] + OMEGA * (face_src[0, -1] - (prev[1, -1] + from_e))
    north_last = face_state[1, :, -1] + OMEGA * (face_src[1, :, -1] - (prev[3, :, -1] + from_n))
    inner = inner.at[-1, 0].set(east_last).at[:, 1, -1].set(north_last)
    face_out = jnp.transpose(
        inner.reshape(tile_rows, 3, tile_cols, trace_width), (0, 2, 1, 3)
    )
    coarse_out = coarse_out.reshape(owner_slots, 1, trace_width)
    return (face_out, coarse_out)


def solution(mesh):
    return jax.shard_map(
        shards,
        mesh=mesh,
        in_specs=(
            P("gx", "gy", None, None),
            P(),
            P("gx", "gy", None, None),
            P("gx", "gy", None),
            P("gx", "gy"),
            P("gx", "gy"),
            P("gx", "gy"),
        ),
        out_specs=(P("gx", "gy", None, None), P("gx", "gy", None)),
        check_vma=False,
    )
```

```python
import jax
import jax.numpy as jnp
from jax import lax
from jax.experimental import pallas as pl
from jax.experimental.pallas import tpu as pltpu
from jax.sharding import PartitionSpec as P

ITERS = 4


OMEGA = 0.8


def extended(cells, sides, width):
    for axis, dim in sides:
        count = lax.axis_size(axis)
        head = lax.slice_in_dim(cells, 0, width, axis=dim)
        tail = lax.slice_in_dim(cells, cells.shape[dim] - width, cells.shape[dim], axis=dim)
        cells = jnp.concatenate(
            [
                lax.ppermute(tail, axis, [(i, (i + 1) % count) for i in range(count)]),
                cells,
                lax.ppermute(head, axis, [((i + 1) % count, i) for i in range(count)]),
            ],
            axis=dim,
        )
    return cells


def to_next(block, axis):
    count = lax.axis_size(axis)
    return lax.ppermute(block, axis, [(i, (i + 1) % count) for i in range(count)])


def to_previous(block, axis):
    count = lax.axis_size(axis)
    return lax.ppermute(block, axis, [((i + 1) % count, i) for i in range(count)])


def apply_update(fs, src, wg, sg, wsrc, ssrc, prev, from_e, from_w, from_n, from_s, fs_o, wg_o, sg_o):
    rows, cols = fs.shape[1], fs.shape[2]
    for i in range(rows):
        neighbour = prev[0, i + 1] if i + 1 < rows else from_e[...]
        fs_o[0, i] = fs[0, i] + OMEGA * (src[0, i] - (prev[1, i] + neighbour))
    for j in range(cols):
        neighbour = prev[2, :, j + 1] if j + 1 < cols else from_n[...]
        fs_o[1, :, j] = fs[1, :, j] + OMEGA * (src[1, :, j] - (prev[3, :, j] + neighbour))
    fs_o[2] = fs[2] + OMEGA * (src[2] - prev[4])
    wg_o[...] = wg[...] + OMEGA * (wsrc[...] - (from_w[...] + prev[0, 0]))
    sg_o[...] = sg[...] + OMEGA * (ssrc[...] - (from_s[...] + prev[2, :, 0]))


def whole(shape):
    return pl.BlockSpec(shape, lambda *_: (0,) * len(shape))


def sweep_call(count, state, src, wsrc, ssrc, top, blocks):
    _, rows, cols, functionals, face_dofs = src.shape
    width = blocks.shape[-1]
    per_step = 2 if rows % 2 == 0 else 1

    def kernel(count_ref, *refs):
        if state is None:
            src_r, wsrc_r, ssrc_r, top_r, b_r = refs[:5]
        else:
            fs_r, wg_r, sg_r, prev_r, fe_r, fw_r, fn_r, fsr_r = refs[:8]
            src_r, wsrc_r, ssrc_r, top_r, b_r = refs[8:13]
        fs_o, wg_o, sg_o, c_o, to_w, to_e, to_s, to_n = refs[-8:]
        step = pl.program_id(0)

        @pl.when(step == 0)
        def _():
            if state is None:
                fs_o[...] = OMEGA * src_r[...]
                wg_o[...] = OMEGA * wsrc_r[...]
                sg_o[...] = OMEGA * ssrc_r[...]
            else:
                apply_update(fs_r, src_r, wg_r, sg_r, wsrc_r, ssrc_r, prev_r, fe_r, fw_r, fn_r,
                             fsr_r, fs_o, wg_o, sg_o)

        for r, j in [(r, j) for r in range(per_step) for j in range(cols)]:
            i = step * per_step + r
            west = jnp.where(i == 0, wg_o[j], fs_o[0, jnp.maximum(i - 1, 0), j])
            south = sg_o[i] if j == 0 else fs_o[1, i, j - 1]
            row = jnp.concatenate(
                [west, fs_o[0, i, j], south, fs_o[1, i, j], fs_o[2, i, j], top_r[i, j]], -1
            )
            out = jnp.dot(row.astype(jnp.bfloat16), b_r[r, j], preferred_element_type=jnp.float32)
            live = ((i * cols + j) < count_ref[0]).astype(jnp.float32)
            out = out * live
            for g in range(6):
                c_o[g, i, j] = out[:, g * face_dofs : (g + 1) * face_dofs]
            if j == 0:
                to_s[i] = out[:, 2 * face_dofs : 3 * face_dofs]
            if j == cols - 1:
                to_n[i] = out[:, 3 * face_dofs : 4 * face_dofs]

        @pl.when(step == 0)
        def _():
            to_w[...] = c_o[0, 0]

        @pl.when(step == rows // per_step - 1)
        def _():
            to_e[...] = c_o[1, rows - 1]

    f32 = jnp.float32
    operands = (() if state is None else tuple(state)) + (src, wsrc, ssrc, top)
    prev = None if state is None else state[3]
    out_shape = (
        jax.ShapeDtypeStruct(src.shape, f32),
        jax.ShapeDtypeStruct(wsrc.shape, f32),
        jax.ShapeDtypeStruct(ssrc.shape, f32),
        jax.ShapeDtypeStruct((6,) + src.shape[1:], f32),
        jax.ShapeDtypeStruct(wsrc.shape, f32),
        jax.ShapeDtypeStruct(wsrc.shape, f32),
        jax.ShapeDtypeStruct(ssrc.shape, f32),
        jax.ShapeDtypeStruct(ssrc.shape, f32),
    )
    specs = [whole(a.shape) for a in operands]
    if state is not None:
        specs[3] = whole((5,) + prev.shape[1:])
    grid_spec = pltpu.PrefetchScalarGridSpec(
        num_scalar_prefetch=1,
        grid=(rows // per_step,),
        in_specs=specs
        + [pl.BlockSpec((per_step, cols, width, width), lambda i, *_: (i, 0, 0, 0))],
        out_specs=[whole(s.shape) for s in out_shape],
    )
    return pl.pallas_call(kernel, grid_spec=grid_spec, out_shape=out_shape)(
        count, *operands, blocks
    )


def final_update(fs, src, prev):
    _, rows, cols, functionals, face_dofs = fs.shape

    def kernel(fs_r, src_r, prev_r, fs_o):
        for i in range(rows):
            if i + 1 < rows:
                fs_o[i, 0] = fs_r[0, i] + OMEGA * (src_r[0, i] - (prev_r[1, i] + prev_r[0, i + 1]))
            else:
                fs_o[i, 0] = fs_r[0, i]
            for j in range(cols):
                if j + 1 < cols:
                    fs_o[i, 1, j] = fs_r[1, i, j] + OMEGA * (
                        src_r[1, i, j] - (prev_r[3, i, j] + prev_r[2, i, j + 1])
                    )
                else:
                    fs_o[i, 1, j] = fs_r[1, i, j]
            fs_o[i, 2] = fs_r[2, i] + OMEGA * (src_r[2, i] - prev_r[4, i])

    return pl.pallas_call(
        kernel,
        grid=(1,),
        in_specs=[whole(fs.shape), whole(src.shape), whole((5,) + prev.shape[1:])],
        out_specs=whole((rows, 3, cols, functionals, face_dofs)),
        out_shape=jax.ShapeDtypeStruct((rows, 3, cols, functionals, face_dofs), jnp.float32),
    )(fs, src, prev)


def patch_shared(inner, east_last, north_last):
    rows, _, cols = inner.shape[:3]

    def kernel(e_ref, n_ref, base_ref, out_ref, sem):
        del base_ref
        east = pltpu.make_async_copy(e_ref, out_ref.at[rows - 1, 0], sem.at[0])
        north = pltpu.make_async_copy(n_ref, out_ref.at[:, 1, cols - 1], sem.at[1])
        east.start()
        north.start()
        east.wait()
        north.wait()

    vmem = pltpu.MemorySpace.VMEM
    return pl.pallas_call(
        kernel,
        in_specs=[
            pl.BlockSpec(memory_space=vmem),
            pl.BlockSpec(memory_space=vmem),
            pl.BlockSpec(memory_space=pl.ANY),
        ],
        out_specs=pl.BlockSpec(memory_space=pl.ANY),
        out_shape=jax.ShapeDtypeStruct(inner.shape, inner.dtype),
        input_output_aliases={2: 0},
        scratch_shapes=[pltpu.SemaphoreType.DMA((2,))],
    )(east_last, north_last, inner)


def shards(
    element_blocks,
    mortar_projection,
    face_sources,
    coarse_sources,
    parent_slot,
    child_position,
    live_count,
):
    highest = lax.Precision.HIGHEST
    tile_rows, tile_cols = parent_slot.shape
    trace_width = face_sources.shape[-1]
    face_dofs = mortar_projection.shape[-1]
    functionals = trace_width // face_dofs
    sources = lax.axis_size("gx")
    owner_slots = coarse_sources.shape[0]
    per_pair = owner_slots // sources
    element_count = tile_rows * tile_cols
    send_slots = sources * per_pair
    count = live_count.reshape(1)
    parents = parent_slot.reshape(element_count)
    positions = child_position.reshape(element_count)
    targets = (
        parents // owner_slots * per_pair + parents % owner_slots - lax.axis_index("gx") * per_pair
    )
    combos = 4 * send_slots
    pair_index = positions * send_slots + targets
    pair_match = pair_index[None, :] == jnp.arange(combos, dtype=jnp.int32)[:, None]
    pair_owner = jnp.sum(
        jnp.where(pair_match, jnp.arange(element_count, dtype=jnp.int32)[None, :], 0), 1
    ) + jnp.where(jnp.any(pair_match, 1), 0, element_count)
    face_src = jnp.moveaxis(
        face_sources.reshape(tile_rows, tile_cols, 3, functionals, face_dofs), 2, 0
    )
    coarse_source = lax.all_to_all(
        coarse_sources[:, 0, :].reshape(sources, per_pair, functionals, face_dofs),
        "gx",
        split_axis=0,
        concat_axis=0,
        tiled=True,
    ).reshape(send_slots, functionals, face_dofs)
    west_source = extended(face_src[0, -1:], (("gx", 0),), 1)[0]
    south_source = extended(face_src[1, :, -1:], (("gy", 1),), 1)[:, 0]

    def coarse_update(coarse_state, prev):
        top_flat = prev[5].reshape(element_count, functionals, face_dofs)
        padded_top = jnp.concatenate(
            [top_flat, jnp.zeros((1, functionals, face_dofs), jnp.float32)], 0
        )
        by_pair = jnp.take(padded_top, pair_owner, axis=0, mode="clip").reshape(
            4, send_slots, functionals, face_dofs
        )
        coarse_sum = jnp.einsum("ptfl,plk->tfk", by_pair, mortar_projection, precision=highest)
        return coarse_state + OMEGA * (coarse_source - coarse_sum)

    state = None
    coarse_state = OMEGA * coarse_source
    for sweep_index in range(1, ITERS):
        if state is not None:
            coarse_state = coarse_update(coarse_state, state[3])
        every_top = jnp.einsum(
            "tfk,plk->ptfl", coarse_state, mortar_projection, precision=highest
        ).reshape(combos, functionals, face_dofs)
        top_face = jnp.take(every_top, pair_index, axis=0, mode="clip").reshape(
            tile_rows, tile_cols, functionals, face_dofs
        )
        face_state, west_ghost, south_ghost, prev, to_w, to_e, to_s, to_n = sweep_call(
            count, state, face_src, west_source, south_source, top_face, element_blocks
        )
        state = (
            face_state,
            west_ghost,
            south_ghost,
            prev,
            to_previous(to_w, "gx"),
            to_next(to_e, "gx"),
            to_previous(to_s, "gy"),
            to_next(to_n, "gy"),
        )
    coarse_state = coarse_update(coarse_state, state[3])
    coarse_out = lax.all_to_all(
        coarse_state.reshape(sources, per_pair, functionals, face_dofs),
        "gx",
        split_axis=0,
        concat_axis=0,
        tiled=True,
    )
    face_state, west_ghost, south_ghost, prev, from_e, from_w, from_n, from_s = state
    inner = final_update(face_state, face_src, prev)
    east_last = face_state[0, -1] + OMEGA * (face_src[0, -1] - (prev[1, -1] + from_e))
    north_last = face_state[1, :, -1] + OMEGA * (face_src[1, :, -1] - (prev[3, :, -1] + from_n))
    inner = patch_shared(inner, east_last, north_last)
    face_out = jnp.transpose(
        inner.reshape(tile_rows, 3, tile_cols, trace_width), (0, 2, 1, 3)
    )
    coarse_out = coarse_out.reshape(owner_slots, 1, trace_width)
    return (face_out, coarse_out)


def solution(mesh):
    return jax.shard_map(
        shards,
        mesh=mesh,
        in_specs=(
            P("gx", "gy", None, None),
            P(),
            P("gx", "gy", None, None),
            P("gx", "gy", None),
            P("gx", "gy"),
            P("gx", "gy"),
            P("gx", "gy"),
        ),
        out_specs=(P("gx", "gy", None, None), P("gx", "gy", None)),
        check_vma=False,
    )
```

```python
import jax
import jax.numpy as jnp
from jax import lax
from jax.experimental import pallas as pl
from jax.experimental.pallas import tpu as pltpu
from jax.sharding import PartitionSpec as P

ITERS = 4


OMEGA = 0.8


def extended(cells, sides, width):
    for axis, dim in sides:
        count = lax.axis_size(axis)
        head = lax.slice_in_dim(cells, 0, width, axis=dim)
        tail = lax.slice_in_dim(cells, cells.shape[dim] - width, cells.shape[dim], axis=dim)
        cells = jnp.concatenate(
            [
                lax.ppermute(tail, axis, [(i, (i + 1) % count) for i in range(count)]),
                cells,
                lax.ppermute(head, axis, [((i + 1) % count, i) for i in range(count)]),
            ],
            axis=dim,
        )
    return cells


def to_next(block, axis):
    count = lax.axis_size(axis)
    return lax.ppermute(block, axis, [(i, (i + 1) % count) for i in range(count)])


def to_previous(block, axis):
    count = lax.axis_size(axis)
    return lax.ppermute(block, axis, [((i + 1) % count, i) for i in range(count)])


def apply_update(fs, src, wg, sg, wsrc, ssrc, prev, from_e, from_w, from_n, from_s, fs_o, wg_o, sg_o):
    rows, cols = fs.shape[1], fs.shape[2]
    for i in range(rows):
        neighbour = prev[0, i + 1] if i + 1 < rows else from_e[...]
        fs_o[0, i] = fs[0, i] + OMEGA * (src[0, i] - (prev[1, i] + neighbour))
    for j in range(cols):
        neighbour = prev[2, :, j + 1] if j + 1 < cols else from_n[...]
        fs_o[1, :, j] = fs[1, :, j] + OMEGA * (src[1, :, j] - (prev[3, :, j] + neighbour))
    fs_o[2] = fs[2] + OMEGA * (src[2] - prev[4])
    wg_o[...] = wg[...] + OMEGA * (wsrc[...] - (from_w[...] + prev[0, 0]))
    sg_o[...] = sg[...] + OMEGA * (ssrc[...] - (from_s[...] + prev[2, :, 0]))


def whole(shape):
    return pl.BlockSpec(shape, lambda *_: (0,) * len(shape))


def sweep_call(count, state, src, wsrc, ssrc, top, blocks):
    _, rows, cols, functionals, face_dofs = src.shape
    width = blocks.shape[-1]
    per_step = 2 if rows % 2 == 0 else 1

    def kernel(count_ref, *refs):
        if state is None:
            src_r, wsrc_r, ssrc_r, top_r, b_r = refs[:5]
        else:
            fs_r, wg_r, sg_r, prev_r, fe_r, fw_r, fn_r, fsr_r = refs[:8]
            src_r, wsrc_r, ssrc_r, top_r, b_r = refs[8:13]
        fs_o, wg_o, sg_o, c_o, to_w, to_e, to_s, to_n = refs[-8:]
        step = pl.program_id(0)

        @pl.when(step == 0)
        def _():
            if state is None:
                fs_o[...] = OMEGA * src_r[...]
                wg_o[...] = OMEGA * wsrc_r[...]
                sg_o[...] = OMEGA * ssrc_r[...]
            else:
                apply_update(fs_r, src_r, wg_r, sg_r, wsrc_r, ssrc_r, prev_r, fe_r, fw_r, fn_r,
                             fsr_r, fs_o, wg_o, sg_o)

        for r, j in [(r, j) for r in range(per_step) for j in range(cols)]:
            i = step * per_step + r
            west = jnp.where(i == 0, wg_o[j], fs_o[0, jnp.maximum(i - 1, 0), j])
            south = sg_o[i] if j == 0 else fs_o[1, i, j - 1]
            row = jnp.concatenate(
                [west, fs_o[0, i, j], south, fs_o[1, i, j], fs_o[2, i, j], top_r[i, j]], -1
            )
            out = jnp.dot(row.astype(jnp.bfloat16), b_r[r, j], preferred_element_type=jnp.float32)
            live = ((i * cols + j) < count_ref[0]).astype(jnp.float32)
            out = out * live
            for g in range(6):
                c_o[g, i, j] = out[:, g * face_dofs : (g + 1) * face_dofs]
            if j == 0:
                to_s[i] = out[:, 2 * face_dofs : 3 * face_dofs]
            if j == cols - 1:
                to_n[i] = out[:, 3 * face_dofs : 4 * face_dofs]

        @pl.when(step == 0)
        def _():
            to_w[...] = c_o[0, 0]

        @pl.when(step == rows // per_step - 1)
        def _():
            to_e[...] = c_o[1, rows - 1]

    f32 = jnp.float32
    operands = (() if state is None else tuple(state)) + (src, wsrc, ssrc, top)
    prev = None if state is None else state[3]
    out_shape = (
        jax.ShapeDtypeStruct(src.shape, f32),
        jax.ShapeDtypeStruct(wsrc.shape, f32),
        jax.ShapeDtypeStruct(ssrc.shape, f32),
        jax.ShapeDtypeStruct((6,) + src.shape[1:], f32),
        jax.ShapeDtypeStruct(wsrc.shape, f32),
        jax.ShapeDtypeStruct(wsrc.shape, f32),
        jax.ShapeDtypeStruct(ssrc.shape, f32),
        jax.ShapeDtypeStruct(ssrc.shape, f32),
    )
    specs = [whole(a.shape) for a in operands]
    if state is not None:
        specs[3] = whole((5,) + prev.shape[1:])
    grid_spec = pltpu.PrefetchScalarGridSpec(
        num_scalar_prefetch=1,
        grid=(rows // per_step,),
        in_specs=specs
        + [pl.BlockSpec((per_step, cols, width, width), lambda i, *_: (i, 0, 0, 0))],
        out_specs=[whole(s.shape) for s in out_shape],
    )
    return pl.pallas_call(kernel, grid_spec=grid_spec, out_shape=out_shape)(
        count, *operands, blocks
    )


def final_update(fs, src, prev):
    _, rows, cols, functionals, face_dofs = fs.shape

    def kernel(fs_r, src_r, prev_r, fs_o):
        for i in range(rows):
            if i + 1 < rows:
                fs_o[i, 0] = fs_r[0, i] + OMEGA * (src_r[0, i] - (prev_r[1, i] + prev_r[0, i + 1]))
            else:
                fs_o[i, 0] = fs_r[0, i]
            for j in range(cols):
                if j + 1 < cols:
                    fs_o[i, 1, j] = fs_r[1, i, j] + OMEGA * (
                        src_r[1, i, j] - (prev_r[3, i, j] + prev_r[2, i, j + 1])
                    )
                else:
                    fs_o[i, 1, j] = fs_r[1, i, j]
            fs_o[i, 2] = fs_r[2, i] + OMEGA * (src_r[2, i] - prev_r[4, i])

    return pl.pallas_call(
        kernel,
        grid=(1,),
        in_specs=[whole(fs.shape), whole(src.shape), whole((5,) + prev.shape[1:])],
        out_specs=whole((rows, 3, cols, functionals, face_dofs)),
        out_shape=jax.ShapeDtypeStruct((rows, 3, cols, functionals, face_dofs), jnp.float32),
    )(fs, src, prev)


def shards(
    element_blocks,
    mortar_projection,
    face_sources,
    coarse_sources,
    parent_slot,
    child_position,
    live_count,
):
    highest = lax.Precision.HIGHEST
    tile_rows, tile_cols = parent_slot.shape
    trace_width = face_sources.shape[-1]
    face_dofs = mortar_projection.shape[-1]
    functionals = trace_width // face_dofs
    sources = lax.axis_size("gx")
    owner_slots = coarse_sources.shape[0]
    per_pair = owner_slots // sources
    element_count = tile_rows * tile_cols
    send_slots = sources * per_pair
    count = live_count.reshape(1)
    parents = parent_slot.reshape(element_count)
    positions = child_position.reshape(element_count)
    targets = (
        parents // owner_slots * per_pair + parents % owner_slots - lax.axis_index("gx") * per_pair
    )
    combos = 4 * send_slots
    pair_index = positions * send_slots + targets
    pair_match = pair_index[None, :] == jnp.arange(combos, dtype=jnp.int32)[:, None]
    pair_owner = jnp.sum(
        jnp.where(pair_match, jnp.arange(element_count, dtype=jnp.int32)[None, :], 0), 1
    ) + jnp.where(jnp.any(pair_match, 1), 0, element_count)
    face_src = jnp.moveaxis(
        face_sources.reshape(tile_rows, tile_cols, 3, functionals, face_dofs), 2, 0
    )
    coarse_source = lax.all_to_all(
        coarse_sources.reshape(sources, per_pair, 1, trace_width),
        "gx",
        split_axis=0,
        concat_axis=0,
        tiled=True,
    ).reshape(send_slots, functionals, face_dofs)
    west_source = extended(face_src[0, -1:], (("gx", 0),), 1)[0]
    south_source = extended(face_src[1, :, -1:], (("gy", 1),), 1)[:, 0]

    def coarse_update(coarse_state, prev):
        top_flat = prev[5].reshape(element_count, functionals, face_dofs)
        padded_top = jnp.concatenate(
            [top_flat, jnp.zeros((1, functionals, face_dofs), jnp.float32)], 0
        )
        by_pair = jnp.take(padded_top, pair_owner, axis=0, mode="clip").reshape(
            4, send_slots, functionals, face_dofs
        )
        coarse_sum = jnp.einsum("ptfl,plk->tfk", by_pair, mortar_projection, precision=highest)
        return coarse_state + OMEGA * (coarse_source - coarse_sum)

    state = None
    coarse_state = OMEGA * coarse_source
    for sweep_index in range(1, ITERS):
        if state is not None:
            coarse_state = coarse_update(coarse_state, state[3])
        every_top = jnp.einsum(
            "tfk,plk->ptfl", coarse_state, mortar_projection, precision=highest
        ).reshape(combos, functionals, face_dofs)
        top_face = jnp.take(every_top, pair_index, axis=0, mode="clip").reshape(
            tile_rows, tile_cols, functionals, face_dofs
        )
        face_state, west_ghost, south_ghost, prev, to_w, to_e, to_s, to_n = sweep_call(
            count, state, face_src, west_source, south_source, top_face, element_blocks
        )
        state = (
            face_state,
            west_ghost,
            south_ghost,
            prev,
            to_previous(to_w, "gx"),
            to_next(to_e, "gx"),
            to_previous(to_s, "gy"),
            to_next(to_n, "gy"),
        )
    coarse_state = coarse_update(coarse_state, state[3])
    coarse_out = lax.all_to_all(
        coarse_state.reshape(sources, per_pair, functionals, face_dofs),
        "gx",
        split_axis=0,
        concat_axis=0,
        tiled=True,
    )
    face_state, west_ghost, south_ghost, prev, from_e, from_w, from_n, from_s = state
    inner = final_update(face_state, face_src, prev)
    east_last = face_state[0, -1] + OMEGA * (face_src[0, -1] - (prev[1, -1] + from_e))
    north_last = face_state[1, :, -1] + OMEGA * (face_src[1, :, -1] - (prev[3, :, -1] + from_n))
    face_out = jnp.transpose(
        inner.reshape(tile_rows, 3, tile_cols, trace_width), (0, 2, 1, 3)
    )
    face_out = face_out.at[-1, :, 0].set(east_last.reshape(tile_cols, trace_width))
    face_out = face_out.at[:, -1, 1].set(north_last.reshape(tile_rows, trace_width))
    coarse_out = coarse_out.reshape(owner_slots, 1, trace_width)
    return (face_out, coarse_out)


def solution(mesh):
    return jax.shard_map(
        shards,
        mesh=mesh,
        in_specs=(
            P("gx", "gy", None, None),
            P(),
            P("gx", "gy", None, None),
            P("gx", "gy", None),
            P("gx", "gy"),
            P("gx", "gy"),
            P("gx", "gy"),
        ),
        out_specs=(P("gx", "gy", None, None), P("gx", "gy", None)),
        check_vma=False,
    )
```

```python
import jax
import jax.numpy as jnp
from jax import lax
from jax.experimental import pallas as pl
from jax.experimental.pallas import tpu as pltpu
from jax.sharding import PartitionSpec as P

ITERS = 4


OMEGA = 0.8


def extended(cells, sides, width):
    for axis, dim in sides:
        count = lax.axis_size(axis)
        head = lax.slice_in_dim(cells, 0, width, axis=dim)
        tail = lax.slice_in_dim(cells, cells.shape[dim] - width, cells.shape[dim], axis=dim)
        cells = jnp.concatenate(
            [
                lax.ppermute(tail, axis, [(i, (i + 1) % count) for i in range(count)]),
                cells,
                lax.ppermute(head, axis, [((i + 1) % count, i) for i in range(count)]),
            ],
            axis=dim,
        )
    return cells


def to_next(block, axis):
    count = lax.axis_size(axis)
    return lax.ppermute(block, axis, [(i, (i + 1) % count) for i in range(count)])


def to_previous(block, axis):
    count = lax.axis_size(axis)
    return lax.ppermute(block, axis, [((i + 1) % count, i) for i in range(count)])


def apply_update(fs, src, wg, sg, wsrc, ssrc, prev, from_e, from_w, from_n, from_s, fs_o, wg_o, sg_o):
    rows, cols = fs.shape[1], fs.shape[2]
    for i in range(rows):
        neighbour = prev[0, i + 1] if i + 1 < rows else from_e[...]
        fs_o[0, i] = fs[0, i] + OMEGA * (src[0, i] - (prev[1, i] + neighbour))
    for j in range(cols):
        neighbour = prev[2, :, j + 1] if j + 1 < cols else from_n[...]
        fs_o[1, :, j] = fs[1, :, j] + OMEGA * (src[1, :, j] - (prev[3, :, j] + neighbour))
    fs_o[2] = fs[2] + OMEGA * (src[2] - prev[4])
    wg_o[...] = wg[...] + OMEGA * (wsrc[...] - (from_w[...] + prev[0, 0]))
    sg_o[...] = sg[...] + OMEGA * (ssrc[...] - (from_s[...] + prev[2, :, 0]))


def whole(shape):
    return pl.BlockSpec(shape, lambda *_: (0,) * len(shape))


def sweep_call(count, state, src, wsrc, ssrc, top, blocks):
    _, rows, cols, functionals, face_dofs = src.shape
    width = blocks.shape[-1]
    per_step = 2 if rows % 2 == 0 else 1

    def kernel(count_ref, *refs):
        if state is None:
            src_r, wsrc_r, ssrc_r, top_r, b_r = refs[:5]
        else:
            fs_r, wg_r, sg_r, prev_r, fe_r, fw_r, fn_r, fsr_r = refs[:8]
            src_r, wsrc_r, ssrc_r, top_r, b_r = refs[8:13]
        fs_o, wg_o, sg_o, c_o, to_w, to_e, to_s, to_n = refs[-8:]
        step = pl.program_id(0)

        @pl.when(step == 0)
        def _():
            if state is None:
                fs_o[...] = OMEGA * src_r[...]
                wg_o[...] = OMEGA * wsrc_r[...]
                sg_o[...] = OMEGA * ssrc_r[...]
            else:
                apply_update(fs_r, src_r, wg_r, sg_r, wsrc_r, ssrc_r, prev_r, fe_r, fw_r, fn_r,
                             fsr_r, fs_o, wg_o, sg_o)

        for r, j in [(r, j) for r in range(per_step) for j in range(cols)]:
            i = step * per_step + r
            west = jnp.where(i == 0, wg_o[j], fs_o[0, jnp.maximum(i - 1, 0), j])
            south = sg_o[i] if j == 0 else fs_o[1, i, j - 1]
            row = jnp.concatenate(
                [west, fs_o[0, i, j], south, fs_o[1, i, j], fs_o[2, i, j], top_r[i, j]], -1
            )
            out = jnp.dot(row.astype(jnp.bfloat16), b_r[r, j], preferred_element_type=jnp.float32)
            live = ((i * cols + j) < count_ref[0]).astype(jnp.float32)
            out = out * live
            for g in range(6):
                c_o[g, i, j] = out[:, g * face_dofs : (g + 1) * face_dofs]
            if j == 0:
                to_s[i] = out[:, 2 * face_dofs : 3 * face_dofs]
            if j == cols - 1:
                to_n[i] = out[:, 3 * face_dofs : 4 * face_dofs]

        @pl.when(step == 0)
        def _():
            to_w[...] = c_o[0, 0]

        @pl.when(step == rows // per_step - 1)
        def _():
            to_e[...] = c_o[1, rows - 1]

    f32 = jnp.float32
    operands = (() if state is None else tuple(state)) + (src, wsrc, ssrc, top)
    prev = None if state is None else state[3]
    out_shape = (
        jax.ShapeDtypeStruct(src.shape, f32),
        jax.ShapeDtypeStruct(wsrc.shape, f32),
        jax.ShapeDtypeStruct(ssrc.shape, f32),
        jax.ShapeDtypeStruct((6,) + src.shape[1:], f32),
        jax.ShapeDtypeStruct(wsrc.shape, f32),
        jax.ShapeDtypeStruct(wsrc.shape, f32),
        jax.ShapeDtypeStruct(ssrc.shape, f32),
        jax.ShapeDtypeStruct(ssrc.shape, f32),
    )
    specs = [whole(a.shape) for a in operands]
    if state is not None:
        specs[3] = whole((5,) + prev.shape[1:])
    grid_spec = pltpu.PrefetchScalarGridSpec(
        num_scalar_prefetch=1,
        grid=(rows // per_step,),
        in_specs=specs
        + [pl.BlockSpec((per_step, cols, width, width), lambda i, *_: (i, 0, 0, 0))],
        out_specs=[whole(s.shape) for s in out_shape],
    )
    return pl.pallas_call(kernel, grid_spec=grid_spec, out_shape=out_shape)(
        count, *operands, blocks
    )


def final_update(fs, src, prev):
    _, rows, cols, functionals, face_dofs = fs.shape

    def kernel(fs_r, src_r, prev_r, fs_o):
        for i in range(rows):
            if i + 1 < rows:
                fs_o[i, 0] = fs_r[0, i] + OMEGA * (src_r[0, i] - (prev_r[1, i] + prev_r[0, i + 1]))
            else:
                fs_o[i, 0] = fs_r[0, i]
            for j in range(cols):
                if j + 1 < cols:
                    fs_o[i, 1, j] = fs_r[1, i, j] + OMEGA * (
                        src_r[1, i, j] - (prev_r[3, i, j] + prev_r[2, i, j + 1])
                    )
                else:
                    fs_o[i, 1, j] = fs_r[1, i, j]
            fs_o[i, 2] = fs_r[2, i] + OMEGA * (src_r[2, i] - prev_r[4, i])

    return pl.pallas_call(
        kernel,
        grid=(1,),
        in_specs=[whole(fs.shape), whole(src.shape), whole((5,) + prev.shape[1:])],
        out_specs=whole((rows, 3, cols, functionals, face_dofs)),
        out_shape=jax.ShapeDtypeStruct((rows, 3, cols, functionals, face_dofs), jnp.float32),
    )(fs, src, prev)


def shards(
    element_blocks,
    mortar_projection,
    face_sources,
    coarse_sources,
    parent_slot,
    child_position,
    live_count,
):
    highest = lax.Precision.HIGHEST
    tile_rows, tile_cols = parent_slot.shape
    trace_width = face_sources.shape[-1]
    face_dofs = mortar_projection.shape[-1]
    functionals = trace_width // face_dofs
    sources = lax.axis_size("gx")
    owner_slots = coarse_sources.shape[0]
    per_pair = owner_slots // sources
    element_count = tile_rows * tile_cols
    send_slots = sources * per_pair
    count = live_count.reshape(1)
    parents = parent_slot.reshape(element_count)
    positions = child_position.reshape(element_count)
    targets = (
        parents // owner_slots * per_pair + parents % owner_slots - lax.axis_index("gx") * per_pair
    )
    combos = 4 * send_slots
    pair_index = positions * send_slots + targets
    pair_match = pair_index[None, :] == jnp.arange(combos, dtype=jnp.int32)[:, None]
    pair_owner = jnp.sum(
        jnp.where(pair_match, jnp.arange(element_count, dtype=jnp.int32)[None, :], 0), 1
    ) + jnp.where(jnp.any(pair_match, 1), 0, element_count)
    face_src = jnp.moveaxis(
        face_sources.reshape(tile_rows, tile_cols, 3, functionals, face_dofs), 2, 0
    )
    coarse_source = lax.all_to_all(
        coarse_sources.reshape(sources, per_pair, 1, trace_width),
        "gx",
        split_axis=0,
        concat_axis=0,
        tiled=True,
    ).reshape(send_slots, functionals, face_dofs)
    west_source = extended(face_src[0, -1:], (("gx", 0),), 1)[0]
    south_source = extended(face_src[1, :, -1:], (("gy", 1),), 1)[:, 0]

    def coarse_update(coarse_state, prev):
        top_flat = prev[5].reshape(element_count, functionals, face_dofs)
        padded_top = jnp.concatenate(
            [top_flat, jnp.zeros((1, functionals, face_dofs), jnp.float32)], 0
        )
        by_pair = jnp.take(padded_top, pair_owner, axis=0, mode="clip").reshape(
            4, send_slots, functionals, face_dofs
        )
        coarse_sum = jnp.einsum("ptfl,plk->tfk", by_pair, mortar_projection, precision=highest)
        return coarse_state + OMEGA * (coarse_source - coarse_sum)

    state = None
    coarse_state = OMEGA * coarse_source
    for sweep_index in range(1, ITERS):
        if state is not None:
            coarse_state = coarse_update(coarse_state, state[3])
        every_top = jnp.einsum(
            "tfk,plk->ptfl", coarse_state, mortar_projection, precision=highest
        ).reshape(combos, functionals, face_dofs)
        top_face = jnp.take(every_top, pair_index, axis=0, mode="clip").reshape(
            tile_rows, tile_cols, functionals, face_dofs
        )
        face_state, west_ghost, south_ghost, prev, to_w, to_e, to_s, to_n = sweep_call(
            count, state, face_src, west_source, south_source, top_face, element_blocks
        )
        state = (
            face_state,
            west_ghost,
            south_ghost,
            prev,
            to_previous(to_w, "gx"),
            to_next(to_e, "gx"),
            to_previous(to_s, "gy"),
            to_next(to_n, "gy"),
        )
    coarse_state = coarse_update(coarse_state, state[3])
    coarse_out = lax.all_to_all(
        coarse_state.reshape(sources, per_pair, functionals, face_dofs),
        "gx",
        split_axis=0,
        concat_axis=0,
        tiled=True,
    )
    face_state, west_ghost, south_ghost, prev, from_e, from_w, from_n, from_s = state
    inner = final_update(face_state, face_src, prev)
    east_last = face_state[0, -1] + OMEGA * (face_src[0, -1] - (prev[1, -1] + from_e))
    north_last = face_state[1, :, -1] + OMEGA * (face_src[1, :, -1] - (prev[3, :, -1] + from_n))
    inner = inner.at[-1, 0].set(east_last).at[:, 1, -1].set(north_last)
    face_out = jnp.transpose(
        inner.reshape(tile_rows, 3, tile_cols, trace_width), (0, 2, 1, 3)
    )
    coarse_out = coarse_out.reshape(owner_slots, 1, trace_width)
    return (face_out, coarse_out)


def solution(mesh):
    return jax.shard_map(
        shards,
        mesh=mesh,
        in_specs=(
            P("gx", "gy", None, None),
            P(),
            P("gx", "gy", None, None),
            P("gx", "gy", None),
            P("gx", "gy"),
            P("gx", "gy"),
            P("gx", "gy"),
        ),
        out_specs=(P("gx", "gy", None, None), P("gx", "gy", None)),
        check_vma=False,
    )
```

```python
import jax
import jax.numpy as jnp
from jax import lax
from jax.experimental import pallas as pl
from jax.experimental.pallas import tpu as pltpu
from jax.sharding import PartitionSpec as P

ITERS = 4


OMEGA = 0.8


def extended(cells, sides, width):
    for axis, dim in sides:
        count = lax.axis_size(axis)
        head = lax.slice_in_dim(cells, 0, width, axis=dim)
        tail = lax.slice_in_dim(cells, cells.shape[dim] - width, cells.shape[dim], axis=dim)
        cells = jnp.concatenate(
            [
                lax.ppermute(tail, axis, [(i, (i + 1) % count) for i in range(count)]),
                cells,
                lax.ppermute(head, axis, [((i + 1) % count, i) for i in range(count)]),
            ],
            axis=dim,
        )
    return cells


def to_next(block, axis):
    count = lax.axis_size(axis)
    return lax.ppermute(block, axis, [(i, (i + 1) % count) for i in range(count)])


def to_previous(block, axis):
    count = lax.axis_size(axis)
    return lax.ppermute(block, axis, [((i + 1) % count, i) for i in range(count)])


def apply_update(fs, src, wg, sg, wsrc, ssrc, prev, from_e, from_w, from_n, from_s, fs_o, wg_o, sg_o):
    rows, cols = fs.shape[1], fs.shape[2]
    for i in range(rows):
        neighbour = prev[0, i + 1] if i + 1 < rows else from_e[...]
        fs_o[0, i] = fs[0, i] + OMEGA * (src[0, i] - (prev[1, i] + neighbour))
    for j in range(cols):
        neighbour = prev[2, :, j + 1] if j + 1 < cols else from_n[...]
        fs_o[1, :, j] = fs[1, :, j] + OMEGA * (src[1, :, j] - (prev[3, :, j] + neighbour))
    fs_o[2] = fs[2] + OMEGA * (src[2] - prev[4])
    wg_o[...] = wg[...] + OMEGA * (wsrc[...] - (from_w[...] + prev[0, 0]))
    sg_o[...] = sg[...] + OMEGA * (ssrc[...] - (from_s[...] + prev[2, :, 0]))


def whole(shape):
    return pl.BlockSpec(shape, lambda *_: (0,) * len(shape))


def sweep_call(count, state, src, wsrc, ssrc, top, blocks):
    _, rows, cols, functionals, face_dofs = src.shape
    width = blocks.shape[-1]
    per_step = 2 if rows % 2 == 0 else 1

    def kernel(count_ref, *refs):
        if state is None:
            src_r, wsrc_r, ssrc_r, top_r, b_r = refs[:5]
        else:
            fs_r, wg_r, sg_r, prev_r, fe_r, fw_r, fn_r, fsr_r = refs[:8]
            src_r, wsrc_r, ssrc_r, top_r, b_r = refs[8:13]
        fs_o, wg_o, sg_o, c_o, to_w, to_e, to_s, to_n = refs[-8:]
        step = pl.program_id(0)

        @pl.when(step == 0)
        def _():
            if state is None:
                fs_o[...] = OMEGA * src_r[...]
                wg_o[...] = OMEGA * wsrc_r[...]
                sg_o[...] = OMEGA * ssrc_r[...]
            else:
                apply_update(fs_r, src_r, wg_r, sg_r, wsrc_r, ssrc_r, prev_r, fe_r, fw_r, fn_r,
                             fsr_r, fs_o, wg_o, sg_o)

        for r, j in [(r, j) for r in range(per_step) for j in range(cols)]:
            i = step * per_step + r
            west = jnp.where(i == 0, wg_o[j], fs_o[0, jnp.maximum(i - 1, 0), j])
            south = sg_o[i] if j == 0 else fs_o[1, i, j - 1]
            row = jnp.concatenate(
                [west, fs_o[0, i, j], south, fs_o[1, i, j], fs_o[2, i, j], top_r[i, j]], -1
            )
            out = jnp.dot(row.astype(jnp.bfloat16), b_r[r, j], preferred_element_type=jnp.float32)
            live = ((i * cols + j) < count_ref[0]).astype(jnp.float32)
            out = out * live
            for g in range(6):
                c_o[g, i, j] = out[:, g * face_dofs : (g + 1) * face_dofs]
            if j == 0:
                to_s[i] = out[:, 2 * face_dofs : 3 * face_dofs]
            if j == cols - 1:
                to_n[i] = out[:, 3 * face_dofs : 4 * face_dofs]

        @pl.when(step == 0)
        def _():
            to_w[...] = c_o[0, 0]

        @pl.when(step == rows // per_step - 1)
        def _():
            to_e[...] = c_o[1, rows - 1]

    f32 = jnp.float32
    operands = (() if state is None else tuple(state)) + (src, wsrc, ssrc, top)
    prev = None if state is None else state[3]
    out_shape = (
        jax.ShapeDtypeStruct(src.shape, f32),
        jax.ShapeDtypeStruct(wsrc.shape, f32),
        jax.ShapeDtypeStruct(ssrc.shape, f32),
        jax.ShapeDtypeStruct((6,) + src.shape[1:], f32),
        jax.ShapeDtypeStruct(wsrc.shape, f32),
        jax.ShapeDtypeStruct(wsrc.shape, f32),
        jax.ShapeDtypeStruct(ssrc.shape, f32),
        jax.ShapeDtypeStruct(ssrc.shape, f32),
    )
    specs = [whole(a.shape) for a in operands]
    if state is not None:
        specs[3] = whole((5,) + prev.shape[1:])
    grid_spec = pltpu.PrefetchScalarGridSpec(
        num_scalar_prefetch=1,
        grid=(rows // per_step,),
        in_specs=specs
        + [pl.BlockSpec((per_step, cols, width, width), lambda i, *_: (i, 0, 0, 0))],
        out_specs=[whole(s.shape) for s in out_shape],
    )
    return pl.pallas_call(kernel, grid_spec=grid_spec, out_shape=out_shape)(
        count, *operands, blocks
    )


def final_update(fs, src, prev):
    _, rows, cols, functionals, face_dofs = fs.shape

    def kernel(fs_r, src_r, prev_r, fs_o):
        for i in range(rows):
            if i + 1 < rows:
                fs_o[i, 0] = fs_r[0, i] + OMEGA * (src_r[0, i] - (prev_r[1, i] + prev_r[0, i + 1]))
            else:
                fs_o[i, 0] = fs_r[0, i]
            for j in range(cols):
                if j + 1 < cols:
                    fs_o[i, 1, j] = fs_r[1, i, j] + OMEGA * (
                        src_r[1, i, j] - (prev_r[3, i, j] + prev_r[2, i, j + 1])
                    )
                else:
                    fs_o[i, 1, j] = fs_r[1, i, j]
            fs_o[i, 2] = fs_r[2, i] + OMEGA * (src_r[2, i] - prev_r[4, i])

    return pl.pallas_call(
        kernel,
        grid=(1,),
        in_specs=[whole(fs.shape), whole(src.shape), whole((5,) + prev.shape[1:])],
        out_specs=whole((rows, 3, cols, functionals, face_dofs)),
        out_shape=jax.ShapeDtypeStruct((rows, 3, cols, functionals, face_dofs), jnp.float32),
    )(fs, src, prev)


def shards(
    element_blocks,
    mortar_projection,
    face_sources,
    coarse_sources,
    parent_slot,
    child_position,
    live_count,
):
    highest = lax.Precision.HIGHEST
    tile_rows, tile_cols = parent_slot.shape
    trace_width = face_sources.shape[-1]
    face_dofs = mortar_projection.shape[-1]
    functionals = trace_width // face_dofs
    sources = lax.axis_size("gx")
    owner_slots = coarse_sources.shape[0]
    per_pair = owner_slots // sources
    element_count = tile_rows * tile_cols
    send_slots = sources * per_pair
    count = live_count.reshape(1)
    parents = parent_slot.reshape(element_count)
    positions = child_position.reshape(element_count)
    targets = (
        parents // owner_slots * per_pair + parents % owner_slots - lax.axis_index("gx") * per_pair
    )
    combos = 4 * send_slots
    pair_index = positions * send_slots + targets
    pair_match = pair_index[None, :] == jnp.arange(combos, dtype=jnp.int32)[:, None]
    pair_owner = jnp.sum(
        jnp.where(pair_match, jnp.arange(element_count, dtype=jnp.int32)[None, :], 0), 1
    ) + jnp.where(jnp.any(pair_match, 1), 0, element_count)
    face_src = jnp.moveaxis(
        face_sources.reshape(tile_rows, tile_cols, 3, functionals, face_dofs), 2, 0
    )
    coarse_source = lax.all_to_all(
        coarse_sources.reshape(sources, per_pair, 1, trace_width),
        "gx",
        split_axis=0,
        concat_axis=0,
        tiled=True,
    ).reshape(send_slots, functionals, face_dofs)
    west_source = extended(face_src[0, -1:], (("gx", 0),), 1)[0]
    south_source = extended(face_src[1, :, -1:], (("gy", 1),), 1)[:, 0]

    def coarse_update(coarse_state, prev):
        top_flat = prev[5].reshape(element_count, functionals, face_dofs)
        padded_top = jnp.concatenate(
            [top_flat, jnp.zeros((1, functionals, face_dofs), jnp.float32)], 0
        )
        by_pair = jnp.take(padded_top, pair_owner, axis=0, mode="clip").reshape(
            4, send_slots, functionals, face_dofs
        )
        coarse_sum = jnp.einsum("ptfl,plk->tfk", by_pair, mortar_projection, precision=highest)
        return coarse_state + OMEGA * (coarse_source - coarse_sum)

    state = None
    coarse_state = OMEGA * coarse_source
    for sweep_index in range(1, ITERS):
        if state is not None:
            coarse_state = coarse_update(coarse_state, state[3])
        every_top = jnp.einsum(
            "tfk,plk->ptfl", coarse_state, mortar_projection, precision=highest
        ).reshape(combos, functionals, face_dofs)
        top_face = jnp.take(every_top, pair_index, axis=0, mode="clip").reshape(
            tile_rows, tile_cols, functionals, face_dofs
        )
        face_state, west_ghost, south_ghost, prev, to_w, to_e, to_s, to_n = sweep_call(
            count, state, face_src, west_source, south_source, top_face, element_blocks
        )
        state = (
            face_state,
            west_ghost,
            south_ghost,
            prev,
            to_previous(to_w, "gx"),
            to_next(to_e, "gx"),
            to_previous(to_s, "gy"),
            to_next(to_n, "gy"),
        )
    coarse_state = coarse_update(coarse_state, state[3])
    coarse_out = lax.all_to_all(
        coarse_state.reshape(sources, per_pair, 1, trace_width),
        "gx",
        split_axis=0,
        concat_axis=0,
        tiled=True,
    )
    face_state, west_ghost, south_ghost, prev, from_e, from_w, from_n, from_s = state
    inner = final_update(face_state, face_src, prev)
    east_last = face_state[0, -1] + OMEGA * (face_src[0, -1] - (prev[1, -1] + from_e))
    north_last = face_state[1, :, -1] + OMEGA * (face_src[1, :, -1] - (prev[3, :, -1] + from_n))
    inner = inner.at[-1, 0].set(east_last).at[:, 1, -1].set(north_last)
    face_out = jnp.transpose(
        inner.reshape(tile_rows, 3, tile_cols, trace_width), (0, 2, 1, 3)
    )
    coarse_out = coarse_out.reshape(owner_slots, 1, trace_width)
    return (face_out, coarse_out)


def solution(mesh):
    return jax.shard_map(
        shards,
        mesh=mesh,
        in_specs=(
            P("gx", "gy", None, None),
            P(),
            P("gx", "gy", None, None),
            P("gx", "gy", None),
            P("gx", "gy"),
            P("gx", "gy"),
            P("gx", "gy"),
        ),
        out_specs=(P("gx", "gy", None, None), P("gx", "gy", None)),
        check_vma=False,
    )
```

```python
import jax
import jax.numpy as jnp
from jax import lax
from jax.experimental import pallas as pl
from jax.experimental.pallas import tpu as pltpu
from jax.sharding import PartitionSpec as P

ITERS = 4


OMEGA = 0.8


def extended(cells, sides, width):
    for axis, dim in sides:
        count = lax.axis_size(axis)
        head = lax.slice_in_dim(cells, 0, width, axis=dim)
        tail = lax.slice_in_dim(cells, cells.shape[dim] - width, cells.shape[dim], axis=dim)
        cells = jnp.concatenate(
            [
                lax.ppermute(tail, axis, [(i, (i + 1) % count) for i in range(count)]),
                cells,
                lax.ppermute(head, axis, [((i + 1) % count, i) for i in range(count)]),
            ],
            axis=dim,
        )
    return cells


def to_next(block, axis):
    count = lax.axis_size(axis)
    return lax.ppermute(block, axis, [(i, (i + 1) % count) for i in range(count)])


def to_previous(block, axis):
    count = lax.axis_size(axis)
    return lax.ppermute(block, axis, [((i + 1) % count, i) for i in range(count)])


def apply_update(fs, src, wg, sg, wsrc, ssrc, prev, from_e, from_w, from_n, from_s, fs_o, wg_o, sg_o):
    rows, cols = fs.shape[1], fs.shape[2]
    for i in range(rows):
        neighbour = prev[0, i + 1] if i + 1 < rows else from_e[...]
        fs_o[0, i] = fs[0, i] + OMEGA * (src[0, i] - (prev[1, i] + neighbour))
    for j in range(cols):
        neighbour = prev[2, :, j + 1] if j + 1 < cols else from_n[...]
        fs_o[1, :, j] = fs[1, :, j] + OMEGA * (src[1, :, j] - (prev[3, :, j] + neighbour))
    fs_o[2] = fs[2] + OMEGA * (src[2] - prev[4])
    wg_o[...] = wg[...] + OMEGA * (wsrc[...] - (from_w[...] + prev[0, 0]))
    sg_o[...] = sg[...] + OMEGA * (ssrc[...] - (from_s[...] + prev[2, :, 0]))


def whole(shape):
    return pl.BlockSpec(shape, lambda *_: (0,) * len(shape))


def sweep_call(count, state, src, wsrc, ssrc, top, blocks):
    _, rows, cols, functionals, face_dofs = src.shape
    width = blocks.shape[-1]
    per_step = 2 if rows % 2 == 0 else 1

    def kernel(count_ref, *refs):
        if state is None:
            src_r, wsrc_r, ssrc_r, top_r, b_r = refs[:5]
        else:
            fs_r, wg_r, sg_r, prev_r, fe_r, fw_r, fn_r, fsr_r = refs[:8]
            src_r, wsrc_r, ssrc_r, top_r, b_r = refs[8:13]
        fs_o, wg_o, sg_o, c_o, to_w, to_e, to_s, to_n = refs[-8:]
        step = pl.program_id(0)

        @pl.when(step == 0)
        def _():
            if state is None:
                fs_o[...] = OMEGA * src_r[...]
                wg_o[...] = OMEGA * wsrc_r[...]
                sg_o[...] = OMEGA * ssrc_r[...]
            else:
                apply_update(fs_r, src_r, wg_r, sg_r, wsrc_r, ssrc_r, prev_r, fe_r, fw_r, fn_r,
                             fsr_r, fs_o, wg_o, sg_o)

        for r, j in [(r, j) for r in range(per_step) for j in range(cols)]:
            i = step * per_step + r
            west = jnp.where(i == 0, wg_o[j], fs_o[0, jnp.maximum(i - 1, 0), j])
            south = sg_o[i] if j == 0 else fs_o[1, i, j - 1]
            row = jnp.concatenate(
                [west, fs_o[0, i, j], south, fs_o[1, i, j], fs_o[2, i, j], top_r[i, j]], -1
            )
            out = jnp.dot(row.astype(jnp.bfloat16), b_r[r, j], preferred_element_type=jnp.float32)
            live = ((i * cols + j) < count_ref[0]).astype(jnp.float32)
            out = out * live
            for g in range(6):
                c_o[g, i, j] = out[:, g * face_dofs : (g + 1) * face_dofs]
            if j == 0:
                to_s[i] = out[:, 2 * face_dofs : 3 * face_dofs]
            if j == cols - 1:
                to_n[i] = out[:, 3 * face_dofs : 4 * face_dofs]

        @pl.when(step == 0)
        def _():
            to_w[...] = c_o[0, 0]

        @pl.when(step == rows // per_step - 1)
        def _():
            to_e[...] = c_o[1, rows - 1]

    f32 = jnp.float32
    operands = (() if state is None else tuple(state)) + (src, wsrc, ssrc, top)
    prev = None if state is None else state[3]
    out_shape = (
        jax.ShapeDtypeStruct(src.shape, f32),
        jax.ShapeDtypeStruct(wsrc.shape, f32),
        jax.ShapeDtypeStruct(ssrc.shape, f32),
        jax.ShapeDtypeStruct((6,) + src.shape[1:], f32),
        jax.ShapeDtypeStruct(wsrc.shape, f32),
        jax.ShapeDtypeStruct(wsrc.shape, f32),
        jax.ShapeDtypeStruct(ssrc.shape, f32),
        jax.ShapeDtypeStruct(ssrc.shape, f32),
    )
    specs = [whole(a.shape) for a in operands]
    if state is not None:
        specs[3] = whole((5,) + prev.shape[1:])
    grid_spec = pltpu.PrefetchScalarGridSpec(
        num_scalar_prefetch=1,
        grid=(rows // per_step,),
        in_specs=specs
        + [pl.BlockSpec((per_step, cols, width, width), lambda i, *_: (i, 0, 0, 0))],
        out_specs=[whole(s.shape) for s in out_shape],
    )
    return pl.pallas_call(kernel, grid_spec=grid_spec, out_shape=out_shape)(
        count, *operands, blocks
    )


def final_update(fs, src, prev):
    _, rows, cols, functionals, face_dofs = fs.shape

    def kernel(fs_r, src_r, prev_r, fs_o):
        for i in range(rows):
            if i + 1 < rows:
                fs_o[i, 0] = fs_r[0, i] + OMEGA * (src_r[0, i] - (prev_r[1, i] + prev_r[0, i + 1]))
            else:
                fs_o[i, 0] = fs_r[0, i]
            for j in range(cols):
                if j + 1 < cols:
                    fs_o[i, 1, j] = fs_r[1, i, j] + OMEGA * (
                        src_r[1, i, j] - (prev_r[3, i, j] + prev_r[2, i, j + 1])
                    )
                else:
                    fs_o[i, 1, j] = fs_r[1, i, j]
            fs_o[i, 2] = fs_r[2, i] + OMEGA * (src_r[2, i] - prev_r[4, i])

    return pl.pallas_call(
        kernel,
        grid=(1,),
        in_specs=[whole(fs.shape), whole(src.shape), whole((5,) + prev.shape[1:])],
        out_specs=whole((rows, 3, cols, functionals, face_dofs)),
        out_shape=jax.ShapeDtypeStruct((rows, 3, cols, functionals, face_dofs), jnp.float32),
    )(fs, src, prev)


def shards(
    element_blocks,
    mortar_projection,
    face_sources,
    coarse_sources,
    parent_slot,
    child_position,
    live_count,
):
    highest = lax.Precision.HIGHEST
    tile_rows, tile_cols = parent_slot.shape
    trace_width = face_sources.shape[-1]
    face_dofs = mortar_projection.shape[-1]
    functionals = trace_width // face_dofs
    sources = lax.axis_size("gx")
    owner_slots = coarse_sources.shape[0]
    per_pair = owner_slots // sources
    element_count = tile_rows * tile_cols
    send_slots = sources * per_pair
    count = live_count.reshape(1)
    parents = parent_slot.reshape(element_count)
    positions = child_position.reshape(element_count)
    targets = (
        parents // owner_slots * per_pair + parents % owner_slots - lax.axis_index("gx") * per_pair
    )
    combos = 4 * send_slots
    pair_index = positions * send_slots + targets
    pair_match = pair_index[None, :] == jnp.arange(combos, dtype=jnp.int32)[:, None]
    pair_owner = jnp.sum(
        jnp.where(pair_match, jnp.arange(element_count, dtype=jnp.int32)[None, :], 0), 1
    ) + jnp.where(jnp.any(pair_match, 1), 0, element_count)
    face_src = jnp.moveaxis(
        face_sources.reshape(tile_rows, tile_cols, 3, functionals, face_dofs), 2, 0
    )
    coarse_source = lax.all_to_all(
        coarse_sources,
        "gx",
        split_axis=0,
        concat_axis=0,
        tiled=True,
    ).reshape(send_slots, functionals, face_dofs)
    west_source = extended(face_src[0, -1:], (("gx", 0),), 1)[0]
    south_source = extended(face_src[1, :, -1:], (("gy", 1),), 1)[:, 0]

    def coarse_update(coarse_state, prev):
        top_flat = prev[5].reshape(element_count, functionals, face_dofs)
        padded_top = jnp.concatenate(
            [top_flat, jnp.zeros((1, functionals, face_dofs), jnp.float32)], 0
        )
        by_pair = jnp.take(padded_top, pair_owner, axis=0, mode="clip").reshape(
            4, send_slots, functionals, face_dofs
        )
        coarse_sum = jnp.einsum("ptfl,plk->tfk", by_pair, mortar_projection, precision=highest)
        return coarse_state + OMEGA * (coarse_source - coarse_sum)

    state = None
    coarse_state = OMEGA * coarse_source
    for sweep_index in range(1, ITERS):
        if state is not None:
            coarse_state = coarse_update(coarse_state, state[3])
        every_top = jnp.einsum(
            "tfk,plk->ptfl", coarse_state, mortar_projection, precision=highest
        ).reshape(combos, functionals, face_dofs)
        top_face = jnp.take(every_top, pair_index, axis=0, mode="clip").reshape(
            tile_rows, tile_cols, functionals, face_dofs
        )
        face_state, west_ghost, south_ghost, prev, to_w, to_e, to_s, to_n = sweep_call(
            count, state, face_src, west_source, south_source, top_face, element_blocks
        )
        state = (
            face_state,
            west_ghost,
            south_ghost,
            prev,
            to_previous(to_w, "gx"),
            to_next(to_e, "gx"),
            to_previous(to_s, "gy"),
            to_next(to_n, "gy"),
        )
    coarse_state = coarse_update(coarse_state, state[3])
    coarse_out = lax.all_to_all(
        coarse_state.reshape(sources, per_pair, functionals, face_dofs),
        "gx",
        split_axis=0,
        concat_axis=0,
        tiled=True,
    )
    face_state, west_ghost, south_ghost, prev, from_e, from_w, from_n, from_s = state
    inner = final_update(face_state, face_src, prev)
    east_last = face_state[0, -1] + OMEGA * (face_src[0, -1] - (prev[1, -1] + from_e))
    north_last = face_state[1, :, -1] + OMEGA * (face_src[1, :, -1] - (prev[3, :, -1] + from_n))
    inner = inner.at[-1, 0].set(east_last).at[:, 1, -1].set(north_last)
    face_out = jnp.transpose(
        inner.reshape(tile_rows, 3, tile_cols, trace_width), (0, 2, 1, 3)
    )
    coarse_out = coarse_out.reshape(owner_slots, 1, trace_width)
    return (face_out, coarse_out)


def solution(mesh):
    return jax.shard_map(
        shards,
        mesh=mesh,
        in_specs=(
            P("gx", "gy", None, None),
            P(),
            P("gx", "gy", None, None),
            P("gx", "gy", None),
            P("gx", "gy"),
            P("gx", "gy"),
            P("gx", "gy"),
        ),
        out_specs=(P("gx", "gy", None, None), P("gx", "gy", None)),
        check_vma=False,
    )
```

```python
import jax
import jax.numpy as jnp
from jax import lax
from jax.experimental import pallas as pl
from jax.experimental.pallas import tpu as pltpu
from jax.sharding import PartitionSpec as P

ITERS = 4


OMEGA = 0.8


def extended(cells, sides, width):
    for axis, dim in sides:
        count = lax.axis_size(axis)
        head = lax.slice_in_dim(cells, 0, width, axis=dim)
        tail = lax.slice_in_dim(cells, cells.shape[dim] - width, cells.shape[dim], axis=dim)
        cells = jnp.concatenate(
            [
                lax.ppermute(tail, axis, [(i, (i + 1) % count) for i in range(count)]),
                cells,
                lax.ppermute(head, axis, [((i + 1) % count, i) for i in range(count)]),
            ],
            axis=dim,
        )
    return cells


def to_next(block, axis):
    count = lax.axis_size(axis)
    return lax.ppermute(block, axis, [(i, (i + 1) % count) for i in range(count)])


def to_previous(block, axis):
    count = lax.axis_size(axis)
    return lax.ppermute(block, axis, [((i + 1) % count, i) for i in range(count)])


def apply_update(fs, src, wg, sg, wsrc, ssrc, prev, from_e, from_w, from_n, from_s, fs_o, wg_o, sg_o):
    rows, cols = fs.shape[1], fs.shape[2]
    for i in range(rows):
        neighbour = prev[0, i + 1] if i + 1 < rows else from_e[...]
        fs_o[0, i] = fs[0, i] + OMEGA * (src[0, i] - (prev[1, i] + neighbour))
    for j in range(cols):
        neighbour = prev[2, :, j + 1] if j + 1 < cols else from_n[...]
        fs_o[1, :, j] = fs[1, :, j] + OMEGA * (src[1, :, j] - (prev[3, :, j] + neighbour))
    fs_o[2] = fs[2] + OMEGA * (src[2] - prev[4])
    wg_o[...] = wg[...] + OMEGA * (wsrc[...] - (from_w[...] + prev[0, 0]))
    sg_o[...] = sg[...] + OMEGA * (ssrc[...] - (from_s[...] + prev[2, :, 0]))


def whole(shape):
    return pl.BlockSpec(shape, lambda *_: (0,) * len(shape))


def sweep_call(count, state, src, wsrc, ssrc, top, blocks):
    _, rows, cols, functionals, face_dofs = src.shape
    width = blocks.shape[-1]
    per_step = 2 if rows % 2 == 0 else 1

    def kernel(count_ref, *refs):
        if state is None:
            src_r, wsrc_r, ssrc_r, top_r, b_r = refs[:5]
        else:
            fs_r, wg_r, sg_r, prev_r, fe_r, fw_r, fn_r, fsr_r = refs[:8]
            src_r, wsrc_r, ssrc_r, top_r, b_r = refs[8:13]
        fs_o, wg_o, sg_o, c_o, to_w, to_e, to_s, to_n = refs[-8:]
        step = pl.program_id(0)

        @pl.when(step == 0)
        def _():
            if state is None:
                fs_o[...] = OMEGA * src_r[...]
                wg_o[...] = OMEGA * wsrc_r[...]
                sg_o[...] = OMEGA * ssrc_r[...]
            else:
                apply_update(fs_r, src_r, wg_r, sg_r, wsrc_r, ssrc_r, prev_r, fe_r, fw_r, fn_r,
                             fsr_r, fs_o, wg_o, sg_o)

        for r, j in [(r, j) for r in range(per_step) for j in range(cols)]:
            i = step * per_step + r
            west = jnp.where(i == 0, wg_o[j], fs_o[0, jnp.maximum(i - 1, 0), j])
            south = sg_o[i] if j == 0 else fs_o[1, i, j - 1]
            row = jnp.concatenate(
                [west, fs_o[0, i, j], south, fs_o[1, i, j], fs_o[2, i, j], top_r[i, j]], -1
            )
            out = jnp.dot(row.astype(jnp.bfloat16), b_r[r, j], preferred_element_type=jnp.float32)
            live = ((i * cols + j) < count_ref[0]).astype(jnp.float32)
            out = out * live
            for g in range(6):
                c_o[g, i, j] = out[:, g * face_dofs : (g + 1) * face_dofs]
            if j == 0:
                to_s[i] = out[:, 2 * face_dofs : 3 * face_dofs]
            if j == cols - 1:
                to_n[i] = out[:, 3 * face_dofs : 4 * face_dofs]

        @pl.when(step == 0)
        def _():
            to_w[...] = c_o[0, 0]

        @pl.when(step == rows // per_step - 1)
        def _():
            to_e[...] = c_o[1, rows - 1]

    f32 = jnp.float32
    operands = (() if state is None else tuple(state)) + (src, wsrc, ssrc, top)
    prev = None if state is None else state[3]
    out_shape = (
        jax.ShapeDtypeStruct(src.shape, f32),
        jax.ShapeDtypeStruct(wsrc.shape, f32),
        jax.ShapeDtypeStruct(ssrc.shape, f32),
        jax.ShapeDtypeStruct((6,) + src.shape[1:], f32),
        jax.ShapeDtypeStruct(wsrc.shape, f32),
        jax.ShapeDtypeStruct(wsrc.shape, f32),
        jax.ShapeDtypeStruct(ssrc.shape, f32),
        jax.ShapeDtypeStruct(ssrc.shape, f32),
    )
    specs = [whole(a.shape) for a in operands]
    if state is not None:
        specs[3] = whole((5,) + prev.shape[1:])
    grid_spec = pltpu.PrefetchScalarGridSpec(
        num_scalar_prefetch=1,
        grid=(rows // per_step,),
        in_specs=specs
        + [pl.BlockSpec((per_step, cols, width, width), lambda i, *_: (i, 0, 0, 0))],
        out_specs=[whole(s.shape) for s in out_shape],
    )
    return pl.pallas_call(kernel, grid_spec=grid_spec, out_shape=out_shape)(
        count, *operands, blocks
    )


def final_update(fs, src, prev):
    _, rows, cols, functionals, face_dofs = fs.shape

    def kernel(fs_r, src_r, prev_r, fs_o):
        for i in range(rows):
            if i + 1 < rows:
                fs_o[i, 0] = fs_r[0, i] + OMEGA * (src_r[0, i] - (prev_r[1, i] + prev_r[0, i + 1]))
            else:
                fs_o[i, 0] = fs_r[0, i]
            for j in range(cols):
                if j + 1 < cols:
                    fs_o[i, 1, j] = fs_r[1, i, j] + OMEGA * (
                        src_r[1, i, j] - (prev_r[3, i, j] + prev_r[2, i, j + 1])
                    )
                else:
                    fs_o[i, 1, j] = fs_r[1, i, j]
            fs_o[i, 2] = fs_r[2, i] + OMEGA * (src_r[2, i] - prev_r[4, i])

    return pl.pallas_call(
        kernel,
        grid=(1,),
        in_specs=[whole(fs.shape), whole(src.shape), whole((5,) + prev.shape[1:])],
        out_specs=whole((rows, 3, cols, functionals, face_dofs)),
        out_shape=jax.ShapeDtypeStruct((rows, 3, cols, functionals, face_dofs), jnp.float32),
    )(fs, src, prev)


def shards(
    element_blocks,
    mortar_projection,
    face_sources,
    coarse_sources,
    parent_slot,
    child_position,
    live_count,
):
    highest = lax.Precision.HIGHEST
    tile_rows, tile_cols = parent_slot.shape
    trace_width = face_sources.shape[-1]
    face_dofs = mortar_projection.shape[-1]
    functionals = trace_width // face_dofs
    sources = lax.axis_size("gx")
    owner_slots = coarse_sources.shape[0]
    per_pair = owner_slots // sources
    element_count = tile_rows * tile_cols
    send_slots = sources * per_pair
    count = live_count.reshape(1)
    parents = parent_slot.reshape(element_count)
    positions = child_position.reshape(element_count)
    targets = (
        parents // owner_slots * per_pair + parents % owner_slots - lax.axis_index("gx") * per_pair
    )
    combos = 4 * send_slots
    pair_index = positions * send_slots + targets
    pair_match = pair_index[None, :] == jnp.arange(combos, dtype=jnp.int32)[:, None]
    pair_owner = jnp.sum(
        jnp.where(pair_match, jnp.arange(element_count, dtype=jnp.int32)[None, :], 0), 1
    ) + jnp.where(jnp.any(pair_match, 1), 0, element_count)
    face_src = jnp.moveaxis(
        face_sources.reshape(tile_rows, tile_cols, 3, functionals, face_dofs), 2, 0
    )
    coarse_source = lax.all_to_all(
        coarse_sources,
        "gx",
        split_axis=0,
        concat_axis=0,
        tiled=True,
    ).reshape(send_slots, functionals, face_dofs)
    west_source = extended(face_src[0, -1:], (("gx", 0),), 1)[0]
    south_source = extended(face_src[1, :, -1:], (("gy", 1),), 1)[:, 0]

    def coarse_update(coarse_state, prev):
        top_flat = prev[5].reshape(element_count, functionals, face_dofs)
        padded_top = jnp.concatenate(
            [top_flat, jnp.zeros((1, functionals, face_dofs), jnp.float32)], 0
        )
        by_pair = jnp.take(padded_top, pair_owner, axis=0, mode="clip").reshape(
            4, send_slots, functionals, face_dofs
        )
        coarse_sum = jnp.einsum("ptfl,plk->tfk", by_pair, mortar_projection, precision=highest)
        return coarse_state + OMEGA * (coarse_source - coarse_sum)

    state = None
    coarse_state = OMEGA * coarse_source
    for sweep_index in range(1, ITERS):
        if state is not None:
            coarse_state = coarse_update(coarse_state, state[3])
        every_top = jnp.einsum(
            "tfk,plk->ptfl", coarse_state, mortar_projection, precision=highest
        ).reshape(combos, functionals, face_dofs)
        top_face = jnp.take(every_top, pair_index, axis=0, mode="clip").reshape(
            tile_rows, tile_cols, functionals, face_dofs
        )
        face_state, west_ghost, south_ghost, prev, to_w, to_e, to_s, to_n = sweep_call(
            count, state, face_src, west_source, south_source, top_face, element_blocks
        )
        state = (
            face_state,
            west_ghost,
            south_ghost,
            prev,
            to_previous(to_w, "gx"),
            to_next(to_e, "gx"),
            to_previous(to_s, "gy"),
            to_next(to_n, "gy"),
        )
    coarse_state = coarse_update(coarse_state, state[3])
    coarse_out = lax.all_to_all(
        coarse_state.reshape(owner_slots, 1, trace_width),
        "gx",
        split_axis=0,
        concat_axis=0,
        tiled=True,
    )
    face_state, west_ghost, south_ghost, prev, from_e, from_w, from_n, from_s = state
    inner = final_update(face_state, face_src, prev)
    east_last = face_state[0, -1] + OMEGA * (face_src[0, -1] - (prev[1, -1] + from_e))
    north_last = face_state[1, :, -1] + OMEGA * (face_src[1, :, -1] - (prev[3, :, -1] + from_n))
    inner = inner.at[-1, 0].set(east_last).at[:, 1, -1].set(north_last)
    face_out = jnp.transpose(
        inner.reshape(tile_rows, 3, tile_cols, trace_width), (0, 2, 1, 3)
    )
    coarse_out = coarse_out.reshape(owner_slots, 1, trace_width)
    return (face_out, coarse_out)


def solution(mesh):
    return jax.shard_map(
        shards,
        mesh=mesh,
        in_specs=(
            P("gx", "gy", None, None),
            P(),
            P("gx", "gy", None, None),
            P("gx", "gy", None),
            P("gx", "gy"),
            P("gx", "gy"),
            P("gx", "gy"),
        ),
        out_specs=(P("gx", "gy", None, None), P("gx", "gy", None)),
        check_vma=False,
    )
```

```python
import jax
import jax.numpy as jnp
from jax import lax
from jax.experimental import pallas as pl
from jax.experimental.pallas import tpu as pltpu
from jax.sharding import PartitionSpec as P

ITERS = 4


OMEGA = 0.8


def extended(cells, sides, width):
    for axis, dim in sides:
        count = lax.axis_size(axis)
        head = lax.slice_in_dim(cells, 0, width, axis=dim)
        tail = lax.slice_in_dim(cells, cells.shape[dim] - width, cells.shape[dim], axis=dim)
        cells = jnp.concatenate(
            [
                lax.ppermute(tail, axis, [(i, (i + 1) % count) for i in range(count)]),
                cells,
                lax.ppermute(head, axis, [((i + 1) % count, i) for i in range(count)]),
            ],
            axis=dim,
        )
    return cells


def to_next(block, axis):
    count = lax.axis_size(axis)
    return lax.ppermute(block, axis, [(i, (i + 1) % count) for i in range(count)])


def to_previous(block, axis):
    count = lax.axis_size(axis)
    return lax.ppermute(block, axis, [((i + 1) % count, i) for i in range(count)])


def apply_update(fs, src, wg, sg, wsrc, ssrc, prev, from_e, from_w, from_n, from_s, fs_o, wg_o, sg_o):
    rows, cols = fs.shape[1], fs.shape[2]
    for i in range(rows):
        neighbour = prev[0, i + 1] if i + 1 < rows else from_e[...]
        fs_o[0, i] = fs[0, i] + OMEGA * (src[0, i] - (prev[1, i] + neighbour))
    for j in range(cols):
        neighbour = prev[2, :, j + 1] if j + 1 < cols else from_n[...]
        fs_o[1, :, j] = fs[1, :, j] + OMEGA * (src[1, :, j] - (prev[3, :, j] + neighbour))
    fs_o[2] = fs[2] + OMEGA * (src[2] - prev[4])
    wg_o[...] = wg[...] + OMEGA * (wsrc[...] - (from_w[...] + prev[0, 0]))
    sg_o[...] = sg[...] + OMEGA * (ssrc[...] - (from_s[...] + prev[2, :, 0]))


def whole(shape):
    return pl.BlockSpec(shape, lambda *_: (0,) * len(shape))


def sweep_call(count, state, src, wsrc, ssrc, top, blocks):
    _, rows, cols, functionals, face_dofs = src.shape
    width = blocks.shape[-1]
    per_step = 3 if rows % 3 == 0 else 1

    def kernel(count_ref, *refs):
        if state is None:
            src_r, wsrc_r, ssrc_r, top_r, b_r = refs[:5]
        else:
            fs_r, wg_r, sg_r, prev_r, fe_r, fw_r, fn_r, fsr_r = refs[:8]
            src_r, wsrc_r, ssrc_r, top_r, b_r = refs[8:13]
        fs_o, wg_o, sg_o, c_o, to_w, to_e, to_s, to_n = refs[-8:]
        step = pl.program_id(0)

        @pl.when(step == 0)
        def _():
            if state is None:
                fs_o[...] = OMEGA * src_r[...]
                wg_o[...] = OMEGA * wsrc_r[...]
                sg_o[...] = OMEGA * ssrc_r[...]
            else:
                apply_update(fs_r, src_r, wg_r, sg_r, wsrc_r, ssrc_r, prev_r, fe_r, fw_r, fn_r,
                             fsr_r, fs_o, wg_o, sg_o)

        for r, j in [(r, j) for r in range(per_step) for j in range(cols)]:
            i = step * per_step + r
            west = jnp.where(i == 0, wg_o[j], fs_o[0, jnp.maximum(i - 1, 0), j])
            south = sg_o[i] if j == 0 else fs_o[1, i, j - 1]
            row = jnp.concatenate(
                [west, fs_o[0, i, j], south, fs_o[1, i, j], fs_o[2, i, j], top_r[i, j]], -1
            )
            out = jnp.dot(row.astype(jnp.bfloat16), b_r[r, j], preferred_element_type=jnp.float32)
            live = ((i * cols + j) < count_ref[0]).astype(jnp.float32)
            out = out * live
            for g in range(6):
                c_o[g, i, j] = out[:, g * face_dofs : (g + 1) * face_dofs]
            if j == 0:
                to_s[i] = out[:, 2 * face_dofs : 3 * face_dofs]
            if j == cols - 1:
                to_n[i] = out[:, 3 * face_dofs : 4 * face_dofs]

        @pl.when(step == 0)
        def _():
            to_w[...] = c_o[0, 0]

        @pl.when(step == rows // per_step - 1)
        def _():
            to_e[...] = c_o[1, rows - 1]

    f32 = jnp.float32
    operands = (() if state is None else tuple(state)) + (src, wsrc, ssrc, top)
    prev = None if state is None else state[3]
    out_shape = (
        jax.ShapeDtypeStruct(src.shape, f32),
        jax.ShapeDtypeStruct(wsrc.shape, f32),
        jax.ShapeDtypeStruct(ssrc.shape, f32),
        jax.ShapeDtypeStruct((6,) + src.shape[1:], f32),
        jax.ShapeDtypeStruct(wsrc.shape, f32),
        jax.ShapeDtypeStruct(wsrc.shape, f32),
        jax.ShapeDtypeStruct(ssrc.shape, f32),
        jax.ShapeDtypeStruct(ssrc.shape, f32),
    )
    specs = [whole(a.shape) for a in operands]
    if state is not None:
        specs[3] = whole((5,) + prev.shape[1:])
    grid_spec = pltpu.PrefetchScalarGridSpec(
        num_scalar_prefetch=1,
        grid=(rows // per_step,),
        in_specs=specs
        + [pl.BlockSpec((per_step, cols, width, width), lambda i, *_: (i, 0, 0, 0))],
        out_specs=[whole(s.shape) for s in out_shape],
    )
    return pl.pallas_call(kernel, grid_spec=grid_spec, out_shape=out_shape)(
        count, *operands, blocks
    )


def final_update(fs, src, prev):
    _, rows, cols, functionals, face_dofs = fs.shape

    def kernel(fs_r, src_r, prev_r, fs_o):
        for i in range(rows):
            if i + 1 < rows:
                fs_o[i, 0] = fs_r[0, i] + OMEGA * (src_r[0, i] - (prev_r[1, i] + prev_r[0, i + 1]))
            else:
                fs_o[i, 0] = fs_r[0, i]
            for j in range(cols):
                if j + 1 < cols:
                    fs_o[i, 1, j] = fs_r[1, i, j] + OMEGA * (
                        src_r[1, i, j] - (prev_r[3, i, j] + prev_r[2, i, j + 1])
                    )
                else:
                    fs_o[i, 1, j] = fs_r[1, i, j]
            fs_o[i, 2] = fs_r[2, i] + OMEGA * (src_r[2, i] - prev_r[4, i])

    return pl.pallas_call(
        kernel,
        grid=(1,),
        in_specs=[whole(fs.shape), whole(src.shape), whole((5,) + prev.shape[1:])],
        out_specs=whole((rows, 3, cols, functionals, face_dofs)),
        out_shape=jax.ShapeDtypeStruct((rows, 3, cols, functionals, face_dofs), jnp.float32),
    )(fs, src, prev)


def shards(
    element_blocks,
    mortar_projection,
    face_sources,
    coarse_sources,
    parent_slot,
    child_position,
    live_count,
):
    highest = lax.Precision.HIGHEST
    tile_rows, tile_cols = parent_slot.shape
    trace_width = face_sources.shape[-1]
    face_dofs = mortar_projection.shape[-1]
    functionals = trace_width // face_dofs
    sources = lax.axis_size("gx")
    owner_slots = coarse_sources.shape[0]
    per_pair = owner_slots // sources
    element_count = tile_rows * tile_cols
    send_slots = sources * per_pair
    count = live_count.reshape(1)
    parents = parent_slot.reshape(element_count)
    positions = child_position.reshape(element_count)
    targets = (
        parents // owner_slots * per_pair + parents % owner_slots - lax.axis_index("gx") * per_pair
    )
    combos = 4 * send_slots
    pair_index = positions * send_slots + targets
    pair_match = pair_index[None, :] == jnp.arange(combos, dtype=jnp.int32)[:, None]
    pair_owner = jnp.sum(
        jnp.where(pair_match, jnp.arange(element_count, dtype=jnp.int32)[None, :], 0), 1
    ) + jnp.where(jnp.any(pair_match, 1), 0, element_count)
    face_src = jnp.moveaxis(
        face_sources.reshape(tile_rows, tile_cols, 3, functionals, face_dofs), 2, 0
    )
    coarse_source = lax.all_to_all(
        coarse_sources,
        "gx",
        split_axis=0,
        concat_axis=0,
        tiled=True,
    ).reshape(send_slots, functionals, face_dofs)
    west_source = extended(face_src[0, -1:], (("gx", 0),), 1)[0]
    south_source = extended(face_src[1, :, -1:], (("gy", 1),), 1)[:, 0]

    def coarse_update(coarse_state, prev):
        top_flat = prev[5].reshape(element_count, functionals, face_dofs)
        padded_top = jnp.concatenate(
            [top_flat, jnp.zeros((1, functionals, face_dofs), jnp.float32)], 0
        )
        by_pair = jnp.take(padded_top, pair_owner, axis=0, mode="clip").reshape(
            4, send_slots, functionals, face_dofs
        )
        coarse_sum = jnp.einsum("ptfl,plk->tfk", by_pair, mortar_projection, precision=highest)
        return coarse_state + OMEGA * (coarse_source - coarse_sum)

    state = None
    coarse_state = OMEGA * coarse_source
    for sweep_index in range(1, ITERS):
        if state is not None:
            coarse_state = coarse_update(coarse_state, state[3])
        every_top = jnp.einsum(
            "tfk,plk->ptfl", coarse_state, mortar_projection, precision=highest
        ).reshape(combos, functionals, face_dofs)
        top_face = jnp.take(every_top, pair_index, axis=0, mode="clip").reshape(
            tile_rows, tile_cols, functionals, face_dofs
        )
        face_state, west_ghost, south_ghost, prev, to_w, to_e, to_s, to_n = sweep_call(
            count, state, face_src, west_source, south_source, top_face, element_blocks
        )
        state = (
            face_state,
            west_ghost,
            south_ghost,
            prev,
            to_previous(to_w, "gx"),
            to_next(to_e, "gx"),
            to_previous(to_s, "gy"),
            to_next(to_n, "gy"),
        )
    coarse_state = coarse_update(coarse_state, state[3])
    coarse_out = lax.all_to_all(
        coarse_state.reshape(sources, per_pair, functionals, face_dofs),
        "gx",
        split_axis=0,
        concat_axis=0,
        tiled=True,
    )
    face_state, west_ghost, south_ghost, prev, from_e, from_w, from_n, from_s = state
    inner = final_update(face_state, face_src, prev)
    east_last = face_state[0, -1] + OMEGA * (face_src[0, -1] - (prev[1, -1] + from_e))
    north_last = face_state[1, :, -1] + OMEGA * (face_src[1, :, -1] - (prev[3, :, -1] + from_n))
    inner = inner.at[-1, 0].set(east_last).at[:, 1, -1].set(north_last)
    face_out = jnp.transpose(
        inner.reshape(tile_rows, 3, tile_cols, trace_width), (0, 2, 1, 3)
    )
    coarse_out = coarse_out.reshape(owner_slots, 1, trace_width)
    return (face_out, coarse_out)


def solution(mesh):
    return jax.shard_map(
        shards,
        mesh=mesh,
        in_specs=(
            P("gx", "gy", None, None),
            P(),
            P("gx", "gy", None, None),
            P("gx", "gy", None),
            P("gx", "gy"),
            P("gx", "gy"),
            P("gx", "gy"),
        ),
        out_specs=(P("gx", "gy", None, None), P("gx", "gy", None)),
        check_vma=False,
    )
```
